256 devices in a mesh: lon: 32 (over y_hi, z, core), lat: 8 (over x, y_lo).
Axes of the slice: x: 4, y: 4 (y_hi: 2, y_lo: 2; y = y_hi * 2 + y_lo), z: 8, core: 2. Of those that a mesh axis runs over, the one named last changes fastest.
Arguments:
- trajectory: float32 [2, 512, 512, 128], P(None, 'lon', 'lat'), may hold values from -4 to 4
- cotangent: float32 [8, 512, 512, 128], P(None, 'lon', 'lat'), may hold values from -6 to 6
- courant: float32 [2, 512, 512, 128], P(None, 'lon', 'lat'), may hold values from -0.5 to 0.5
- branch: int32 [512, 512, 128], P('lon', 'lat'), may hold values from 0 to 3
- cloud_list: int32 [32, 8, 768], P('lon', 'lat'), may hold values from 0 to 1023, as said below
- cloud_count: int32 [32, 8], P('lon', 'lat'), may hold values from 0 to 768, as said below
Outputs:
- adjoint_state: float32 [8, 512, 512, 128], P(None, 'lon', 'lat')
The draws below stay inside these ranges and needn't reach their ends.
Inputs may be any that keep to these rules, and one draw needn't show every extreme that they name: `cloud_count`: for every lat index, the counts of the 32 devices of that lon cycle add up to 8192. `cloud_list`: each device's entries are distinct local column numbers.
All inputs are finite; a program needn't handle non-finite values.
Results may differ from the reference program's by a relative error of at most 0.0003.
Values sent between devices are 32-bit elements; how exact they have to be, the bound alone decides.
No kernel may reach another device: no remote copies, remote signals or barrier semaphores. Data moves between devices by JAX's collectives and lax.ppermute only.
A program may use at most 64 MiB of HBM per device.

```python
import jax
import jax.numpy as jnp
from jax import lax

CLON = 16
CLAT = 64
LEV = 128
FIELDS = 8
NEWT = 4
MEAN = 256
CAP = 768
NLON = 512
NLAT = 512
N_LON = 32
N_LAT = 8


def draw_cloud_count(key, part):
    first_key = jax.random.fold_in(key, 11)
    second_key = jax.random.fold_in(key, 12)
    third_key = jax.random.fold_in(key, 13)
    halves = N_LON // 2
    lifted = jax.random.randint(first_key, (N_LAT, halves), 0, MEAN // 2 + 1)
    chosen = jax.random.randint(second_key, (N_LAT, 1), 0, halves)
    spot = jnp.arange(halves, dtype=jnp.int32)[None, :]
    distance = (spot - chosen) % halves
    lifted = jnp.where(distance == 0, MEAN, jnp.where((distance == 1) | (distance == halves - 1), 0, lifted))
    even_counts = MEAN + 2 * lifted
    odd_counts = MEAN - lifted - jnp.roll(lifted, -1, axis=1)
    cycle = jnp.stack([even_counts, odd_counts], -1).reshape(N_LAT, N_LON)
    row_keys = jax.random.split(third_key, N_LAT)

    def shuffle(row_key, row):
        return row[jax.random.permutation(row_key, N_LON)]
    mixed_rows = jax.vmap(shuffle)(row_keys, cycle)
    return jnp.transpose(mixed_rows).astype(jnp.int32)


def draw_cloud_list(key, part):
    base_key = jax.random.fold_in(key, 21)
    keys = jax.random.split(base_key, N_LON * N_LAT)

    def one_device(device_key):
        return jax.random.permutation(device_key, CLON * CLAT)[:CAP]
    lists = jax.vmap(one_device)(keys)
    return lists.reshape(N_LON, N_LAT, CAP).astype(jnp.int32)


def touch_ends(entries, own_key, smallest, top_value):
    spot = [jax.random.randint(jax.random.fold_in(own_key, axis), (), 0, length) for axis, length in enumerate(entries.shape)]
    main_axis = entries.shape.index(max(entries.shape))
    neighbour = spot[:main_axis] + [(spot[main_axis] + 1) % entries.shape[main_axis]] + spot[main_axis + 1:]
    return entries.at[tuple(spot)].set(smallest).at[tuple(neighbour)].set(top_value)


def steps_of(stream_key, dims, cuts, least, top_value):
    gain = 1.0
    for dim, shards_of in cuts:
        steps = jax.random.uniform(jax.random.fold_in(jax.random.fold_in(stream_key, 6), dim), (shards_of,), jnp.float32, least / len(cuts), top_value / len(cuts))
        gain = gain * jnp.repeat(jnp.exp(steps), dims[dim] // shards_of).reshape((-1,) + (1,) * (len(dims) - 1 - dim))
    return gain


def noise(own_key, dims, width, reach, cuts=(), kind=jnp.bfloat16):
    gain = steps_of(own_key, dims, cuts, -0.22, 0.18) if cuts else 1.0
    entries = jax.random.normal(own_key, dims, jnp.float32) * width * gain
    return jnp.minimum(jnp.maximum(entries, -reach), reach).astype(kind)


def setup_inputs(seed: int = 0) -> dict:
    key_list = jax.random.split(jax.random.key(seed), 7)
    return {
        "trajectory": noise(key_list[0], (2, NLON, NLAT, LEV), 1.0, 4.0, ((1, 32), (2, 8)), jnp.float32),
        "cotangent": noise(key_list[1], (FIELDS, NLON, NLAT, LEV), 1.0, 6.0, ((1, 32), (2, 8)), jnp.float32),
        "courant": jnp.clip(jax.random.uniform(key_list[2], (2, NLON, NLAT, LEV), jnp.float32, -0.5, 0.5) * steps_of(key_list[2], (2, NLON, NLAT, LEV), ((1, 32), (2, 8)), -0.4, 0.0), -0.5, 0.5),
        "branch": touch_ends(jax.random.randint(key_list[3], (NLON, NLAT, LEV), 0, 4), jax.random.fold_in(key_list[3], 1), 0, 3).astype(jnp.int32),
        "cloud_list": draw_cloud_list(jax.random.fold_in(key_list[6], 71), 0),
        "cloud_count": draw_cloud_count(jax.random.fold_in(key_list[6], 71), 0),
    }


growth = 0.5
latent_liquid = 1.0
latent_ice = 1.3

def increments(warmth, vapour, kinds):
    mixed = jax.nn.sigmoid(2.0 * warmth)
    liquid_share = jnp.where(kinds == 1, 1.0, jnp.where(kinds == 2, 0.0, mixed))
    latent = latent_liquid * liquid_share + latent_ice * (1.0 - liquid_share)
    active = (kinds > 0).astype(warmth.dtype)
    amount = jnp.zeros_like(warmth)
    for newton_step in range(NEWT):
        saturated = jnp.exp(growth * (warmth + latent * amount))
        excess = vapour - amount - saturated
        amount = amount + excess / (1.0 + growth * latent * saturated)
    amount = active * amount
    return (latent * amount, -amount, liquid_share * amount, (1.0 - liquid_share) * amount)

def sat_adjoint(warmth, vapour, kinds, cot_heat, cot_vapour, cot_liquid, cot_ice):

    def forward(first_in, second_in):
        return increments(first_in, second_in, kinds)
    unused, pullback = jax.vjp(forward, warmth, vapour)
    grad_heat, grad_vapour = pullback((cot_heat, cot_vapour, cot_liquid, cot_ice))
    return (cot_heat + grad_heat, cot_vapour + grad_vapour)

def centred(padded, dim, count):

    def part(start):
        return lax.slice_in_dim(padded, start, start + count, axis=dim)
    return (8.0 * (part(3) - part(1)) - (part(4) - part(0))) / 12.0

def blocks(array):
    lead = array.shape[:-3]
    shaped = array.reshape(lead + (N_LON, CLON, N_LAT, CLAT, LEV))
    depth = len(lead)
    order = tuple(range(depth)) + (depth, depth + 2, depth + 1, depth + 3, depth + 4)
    return jnp.transpose(shaped, order).reshape(lead + (N_LON, N_LAT, CLON * CLAT, LEV))

def unblock(array):
    lead = array.shape[:-4]
    shaped = array.reshape(lead + (N_LON, N_LAT, CLON, CLAT, LEV))
    depth = len(lead)
    order = tuple(range(depth)) + (depth, depth + 2, depth + 1, depth + 3, depth + 4)
    return jnp.transpose(shaped, order).reshape(lead + (NLON, NLAT, LEV))

def pick(array, index):
    wanted = jnp.broadcast_to(index[..., None], array.shape[:-2] + (CAP, LEV))
    return jnp.take_along_axis(array, wanted, axis=-2)

def place(base_block, index, values):
    return base_block.at[:, index].set(values)

def advect_adjoint(field, lon_courant, lat_courant):
    lon_padded = jnp.pad(lon_courant * field, ((2, 2), (0, 0), (0, 0)), mode='wrap')
    lat_padded = jnp.pad(lat_courant * field, ((0, 0), (2, 2), (0, 0)))
    return field + centred(lon_padded, 0, NLON) + centred(lat_padded, 1, NLAT)

def reference(trajectory, cotangent, courant, branch, cloud_list, cloud_count):
    index = cloud_list.astype(jnp.int32)
    moist = pick(blocks(cotangent[:4]), index)
    states = pick(blocks(trajectory), index)
    kinds = pick(blocks(branch), index)
    new_heat, new_vapour = sat_adjoint(states[0], states[1], kinds, moist[0], moist[1], moist[2], moist[3])
    valid = (jnp.arange(CAP, dtype=jnp.int32)[None, None, :] < cloud_count[:, :, None])[..., None]
    new_heat = jnp.where(valid, new_heat, moist[0])
    new_vapour = jnp.where(valid, new_vapour, moist[1])
    fresh = jnp.moveaxis(jnp.stack([new_heat, new_vapour]), 0, 2)
    base = jnp.moveaxis(blocks(cotangent[:2]), 0, 2)
    updated = jax.vmap(jax.vmap(place))(base, index, fresh)
    first = unblock(jnp.moveaxis(updated, 2, 0))
    after = jnp.concatenate([first, cotangent[2:]], 0)
    return lax.map(lambda field: advect_adjoint(field, courant[0], courant[1]), after)
```

```python
import jax
import jax.numpy as jnp
from jax import lax
from jax.sharding import PartitionSpec as P

NEWT = 4


growth = 0.5
latent_liquid = 1.0
latent_ice = 1.3


def with_halo(block, sides, width, periodic):
    for axis, dim in sides:
        count = lax.axis_size(axis)
        forward = [(i, i + 1) for i in range(count - 1)]
        if periodic:
            forward.append((count - 1, 0))
        backward = [(target, source) for source, target in forward]
        low = lax.ppermute(
            lax.slice_in_dim(block, block.shape[dim] - width, None, axis=dim), axis, forward
        )
        high = lax.ppermute(lax.slice_in_dim(block, 0, width, axis=dim), axis, backward)
        block = jnp.concatenate([low, block, high], axis=dim)
    return block


def increments(warmth, vapour, kinds):
    mixed = jax.nn.sigmoid(2.0 * warmth)
    liquid_share = jnp.where(kinds == 1, 1.0, jnp.where(kinds == 2, 0.0, mixed))
    latent = latent_liquid * liquid_share + latent_ice * (1.0 - liquid_share)
    active = (kinds > 0).astype(warmth.dtype)
    amount = jnp.zeros_like(warmth)
    for newton_step in range(NEWT):
        saturated = jnp.exp(growth * (warmth + latent * amount))
        excess = vapour - amount - saturated
        amount = amount + excess / (1.0 + growth * latent * saturated)
    amount = active * amount
    return (latent * amount, -amount, liquid_share * amount, (1.0 - liquid_share) * amount)


def sat_adjoint(warmth, vapour, kinds, cot_heat, cot_vapour, cot_liquid, cot_ice):

    def forward(first_in, second_in):
        return increments(first_in, second_in, kinds)

    unused, pullback = jax.vjp(forward, warmth, vapour)
    grad_heat, grad_vapour = pullback((cot_heat, cot_vapour, cot_liquid, cot_ice))
    return (cot_heat + grad_heat, cot_vapour + grad_vapour)


def centred(padded, dim, count):

    def part(start):
        return lax.slice_in_dim(padded, start, start + count, axis=dim)

    return (8.0 * (part(3) - part(1)) - (part(4) - part(0))) / 12.0


def cloudy_columns(cloud_list, cloud_count, columns):
    index = cloud_list[0, 0]
    count = cloud_count[0, 0]
    slot = jnp.arange(index.shape[0], dtype=jnp.int32)
    hit = (index[:, None] == jnp.arange(columns, dtype=jnp.int32)[None, :]) & (slot < count)[:, None]
    return jnp.any(hit, axis=0)


def on_device(trajectory, cotangent, courant, branch, cloud_list, cloud_count):
    fields, local_lon, local_lat, levels = cotangent.shape
    cloudy = cloudy_columns(cloud_list, cloud_count, local_lon * local_lat)
    cloudy = cloudy.reshape(local_lon, local_lat, 1)
    new_heat, new_vapour = sat_adjoint(
        trajectory[0],
        trajectory[1],
        branch,
        cotangent[0],
        cotangent[1],
        cotangent[2],
        cotangent[3],
    )
    first = jnp.stack(
        [jnp.where(cloudy, new_heat, cotangent[0]), jnp.where(cloudy, new_vapour, cotangent[1])]
    )
    after = jnp.concatenate([first, cotangent[2:]], 0)
    weighted_lon = courant[0] * after
    weighted_lat = courant[1] * after
    lon_part = with_halo(weighted_lon, (("lon", 1),), 2, True)
    lat_part = with_halo(weighted_lat, (("lat", 2),), 2, False)
    return after + centred(lon_part, 1, local_lon) + centred(lat_part, 2, local_lat)


def solution(mesh):
    placed = (
        P(None, "lon", "lat", None),
        P(None, "lon", "lat", None),
        P(None, "lon", "lat", None),
        P("lon", "lat", None),
        P("lon", "lat", None),
        P("lon", "lat"),
    )
    return jax.shard_map(
        on_device,
        mesh=mesh,
        in_specs=placed,
        out_specs=P(None, "lon", "lat", None),
        check_vma=False,
    )
```

```python
import jax
import jax.numpy as jnp
from jax import lax
from jax.sharding import PartitionSpec as P

NEWT = 4


growth = 0.5
latent_liquid = 1.0
latent_ice = 1.3


def increments(warmth, vapour, kinds):
    mixed = jax.nn.sigmoid(2.0 * warmth)
    liquid_share = jnp.where(kinds == 1, 1.0, jnp.where(kinds == 2, 0.0, mixed))
    latent = latent_liquid * liquid_share + latent_ice * (1.0 - liquid_share)
    active = (kinds > 0).astype(warmth.dtype)
    amount = jnp.zeros_like(warmth)
    for newton_step in range(NEWT):
        saturated = jnp.exp(growth * (warmth + latent * amount))
        excess = vapour - amount - saturated
        amount = amount + excess / (1.0 + growth * latent * saturated)
    amount = active * amount
    return (latent * amount, -amount, liquid_share * amount, (1.0 - liquid_share) * amount)


def sat_adjoint(warmth, vapour, kinds, cot_heat, cot_vapour, cot_liquid, cot_ice):

    def forward(first_in, second_in):
        return increments(first_in, second_in, kinds)

    unused, pullback = jax.vjp(forward, warmth, vapour)
    grad_heat, grad_vapour = pullback((cot_heat, cot_vapour, cot_liquid, cot_ice))
    return (cot_heat + grad_heat, cot_vapour + grad_vapour)


def centred(padded, dim, count):

    def part(start):
        return lax.slice_in_dim(padded, start, start + count, axis=dim)

    return (8.0 * (part(3) - part(1)) - (part(4) - part(0))) / 12.0


def zero_padded_centred(field, dim):
    widths = [(0, 0)] * field.ndim
    widths[dim] = (2, 2)
    return centred(jnp.pad(field, widths), dim, field.shape[dim])


def cloudy_columns(cloud_list, cloud_count, columns):
    index = cloud_list[0, 0]
    count = cloud_count[0, 0]
    slot = jnp.arange(index.shape[0], dtype=jnp.int32)
    hit = (index[:, None] == jnp.arange(columns, dtype=jnp.int32)[None, :]) & (slot < count)[:, None]
    return jnp.any(hit, axis=0)


def first_pair(trajectory, cotangent, branch, cloudy):
    new_heat, new_vapour = sat_adjoint(
        trajectory[0],
        trajectory[1],
        branch,
        cotangent[0],
        cotangent[1],
        cotangent[2],
        cotangent[3],
    )
    return jnp.stack(
        [jnp.where(cloudy, new_heat, cotangent[0]), jnp.where(cloudy, new_vapour, cotangent[1])]
    )


def edge(array, dim, start, width=2):
    return lax.slice_in_dim(array, start, start + width, axis=dim)


def edge_after(trajectory, cotangent, branch, cloudy, dim, start):
    sub = lambda a, d: edge(a, d, start)
    pair = first_pair(sub(trajectory, dim), sub(cotangent[:4], dim), sub(branch, dim - 1), sub(cloudy, dim - 1))
    return jnp.concatenate([pair, sub(cotangent[2:], dim)], 0)


def exchange(trajectory, cotangent, courant, branch, cloudy, axis, dim, periodic):
    size = cotangent.shape[dim]
    count = lax.axis_size(axis)
    forward = [(i, i + 1) for i in range(count - 1)]
    if periodic:
        forward.append((count - 1, 0))
    backward = [(target, source) for source, target in forward]
    weight = courant[dim - 1]
    top = edge(weight, dim - 1, size - 2) * edge_after(trajectory, cotangent, branch, cloudy, dim, size - 2)
    bottom = edge(weight, dim - 1, 0) * edge_after(trajectory, cotangent, branch, cloudy, dim, 0)
    low = lax.ppermute(top, axis, forward)
    high = lax.ppermute(bottom, axis, backward)
    return low, high


def add_halo(out, low, high, dim):
    size = out.shape[dim]
    row = lambda a, i: lax.slice_in_dim(a, i, i + 1, axis=dim)
    first = jnp.concatenate(
        [(row(low, 0) - 8.0 * row(low, 1)) / 12.0, row(low, 1) / 12.0], dim
    )
    last = jnp.concatenate(
        [-row(high, 0) / 12.0, (8.0 * row(high, 0) - row(high, 1)) / 12.0], dim
    )
    out = lax.dynamic_update_slice_in_dim(out, edge(out, dim, 0) + first, 0, dim)
    out = lax.dynamic_update_slice_in_dim(out, edge(out, dim, size - 2) + last, size - 2, dim)
    return out


def on_device(trajectory, cotangent, courant, branch, cloud_list, cloud_count):
    fields, local_lon, local_lat, levels = cotangent.shape
    cloudy = cloudy_columns(cloud_list, cloud_count, local_lon * local_lat)
    cloudy = cloudy.reshape(local_lon, local_lat, 1)
    lon_low, lon_high = exchange(trajectory, cotangent, courant, branch, cloudy, "lon", 1, True)
    lat_low, lat_high = exchange(trajectory, cotangent, courant, branch, cloudy, "lat", 2, False)
    after = jnp.concatenate([first_pair(trajectory, cotangent[:4], branch, cloudy), cotangent[2:]], 0)
    out = after + zero_padded_centred(courant[0] * after, 1) + zero_padded_centred(courant[1] * after, 2)
    out = add_halo(out, lon_low, lon_high, 1)
    out = add_halo(out, lat_low, lat_high, 2)
    return out


def solution(mesh):
    placed = (
        P(None, "lon", "lat", None),
        P(None, "lon", "lat", None),
        P(None, "lon", "lat", None),
        P("lon", "lat", None),
        P("lon", "lat", None),
        P("lon", "lat"),
    )
    return jax.shard_map(
        on_device,
        mesh=mesh,
        in_specs=placed,
        out_specs=P(None, "lon", "lat", None),
        check_vma=False,
    )
```

```python
import jax
import jax.numpy as jnp
from jax import lax
from jax.experimental import pallas as pl
from jax.experimental.pallas import tpu as pltpu
from jax.sharding import PartitionSpec as P

NEWT = 4


growth = 0.5
latent_liquid = 1.0
latent_ice = 1.3


def increments(warmth, vapour, kinds):
    mixed = jax.nn.sigmoid(2.0 * warmth)
    liquid_share = jnp.where(kinds == 1, 1.0, jnp.where(kinds == 2, 0.0, mixed))
    latent = latent_liquid * liquid_share + latent_ice * (1.0 - liquid_share)
    active = (kinds > 0).astype(warmth.dtype)
    amount = jnp.zeros_like(warmth)
    for newton_step in range(NEWT):
        saturated = jnp.exp(growth * (warmth + latent * amount))
        excess = vapour - amount - saturated
        amount = amount + excess / (1.0 + growth * latent * saturated)
    amount = active * amount
    return (latent * amount, -amount, liquid_share * amount, (1.0 - liquid_share) * amount)


def sat_adjoint(warmth, vapour, kinds, cot_heat, cot_vapour, cot_liquid, cot_ice):

    def forward(first_in, second_in):
        return increments(first_in, second_in, kinds)

    unused, pullback = jax.vjp(forward, warmth, vapour)
    grad_heat, grad_vapour = pullback((cot_heat, cot_vapour, cot_liquid, cot_ice))
    return (cot_heat + grad_heat, cot_vapour + grad_vapour)


def cloudy_columns(cloud_list, cloud_count, columns):
    index = cloud_list[0, 0]
    count = cloud_count[0, 0]
    slot = jnp.arange(index.shape[0], dtype=jnp.int32)
    hit = (index[:, None] == jnp.arange(columns, dtype=jnp.int32)[None, :]) & (slot < count)[:, None]
    return jnp.any(hit, axis=0)


def sat_kernel(traj_ref, cot_ref, kind_ref, mask_ref, out_ref):
    rows = traj_ref.shape[1]
    tiles = traj_ref.shape[2] // 8

    def step(i, carry):
        r = i // tiles
        lat = pl.ds(pl.multiple_of((i % tiles) * 8, 8), 8)
        cot = [cot_ref[k, r, lat, :] for k in range(4)]
        new_heat, new_vapour = sat_adjoint(
            traj_ref[0, r, lat, :], traj_ref[1, r, lat, :], kind_ref[r, lat, :], *cot
        )
        cloudy = mask_ref[r, lat, :] > 0.0
        out_ref[0, r, lat, :] = jnp.where(cloudy, new_heat, cot[0])
        out_ref[1, r, lat, :] = jnp.where(cloudy, new_vapour, cot[1])
        return carry

    lax.fori_loop(0, rows * tiles, step, 0)


def first_pair(trajectory, cotangent, branch, mask):
    _, nlon, nlat, lev = trajectory.shape
    rows = 4
    return pl.pallas_call(
        sat_kernel,
        grid=(nlon // rows,),
        in_specs=[
            pl.BlockSpec((2, rows, nlat, lev), lambda i: (0, i, 0, 0)),
            pl.BlockSpec((4, rows, nlat, lev), lambda i: (0, i, 0, 0)),
            pl.BlockSpec((rows, nlat, lev), lambda i: (i, 0, 0)),
            pl.BlockSpec((rows, nlat, lev), lambda i: (i, 0, 0)),
        ],
        out_specs=pl.BlockSpec((2, rows, nlat, lev), lambda i: (0, i, 0, 0)),
        out_shape=jax.ShapeDtypeStruct((2, nlon, nlat, lev), jnp.float32),
    )(trajectory, cotangent, branch, mask)


def stencil_kernel(first_ref, cot_ref, cour_ref, lon_low, lon_high, lat_low, lat_high, out_ref, lon_pad, lat_pad):
    nlon, nlat = out_ref.shape[1], out_ref.shape[2]
    f = pl.program_id(0)

    def compute(src):
        for r in range(nlon):
            lon_pad[r + 2] = cour_ref[0, r] * src[0, r]
        lon_pad[0:2] = lon_low[0]
        lon_pad[nlon + 2:nlon + 4] = lon_high[0]
        for r in range(nlon):
            lat_pad[8:8 + nlat] = cour_ref[1, r] * src[0, r]
            lat_pad[6:8] = lat_low[0, 2 * r:2 * r + 2]
            lat_pad[8 + nlat:10 + nlat] = lat_high[0, 2 * r:2 * r + 2]
            d_lat = (8.0 * (lat_pad[9:9 + nlat] - lat_pad[7:7 + nlat]) - (lat_pad[10:10 + nlat] - lat_pad[6:6 + nlat])) / 12.0
            d_lon = (8.0 * (lon_pad[r + 3] - lon_pad[r + 1]) - (lon_pad[r + 4] - lon_pad[r])) / 12.0
            out_ref[0, r] = src[0, r] + d_lon + d_lat

    @pl.when(f < 2)
    def _():
        compute(first_ref)

    @pl.when(f >= 2)
    def _():
        compute(cot_ref)


def advect(first, cotangent, courant, lon_low, lon_high, lat_low, lat_high):
    fields, nlon, nlat, lev = cotangent.shape
    return pl.pallas_call(
        stencil_kernel,
        grid=(fields,),
        in_specs=[
            pl.BlockSpec((1, nlon, nlat, lev), lambda f: (jnp.minimum(f, 1), 0, 0, 0)),
            pl.BlockSpec((1, nlon, nlat, lev), lambda f: (f, 0, 0, 0)),
            pl.BlockSpec((2, nlon, nlat, lev), lambda f: (0, 0, 0, 0)),
            pl.BlockSpec((1, 2, nlat, lev), lambda f: (f, 0, 0, 0)),
            pl.BlockSpec((1, 2, nlat, lev), lambda f: (f, 0, 0, 0)),
            pl.BlockSpec((1, 2 * nlon, lev), lambda f: (f, 0, 0)),
            pl.BlockSpec((1, 2 * nlon, lev), lambda f: (f, 0, 0)),
        ],
        out_specs=pl.BlockSpec((1, nlon, nlat, lev), lambda f: (f, 0, 0, 0)),
        out_shape=jax.ShapeDtypeStruct(cotangent.shape, jnp.float32),
        scratch_shapes=[
            pltpu.VMEM((nlon + 4, nlat, lev), jnp.float32),
            pltpu.VMEM((nlat + 16, lev), jnp.float32),
        ],
    )(first, cotangent, courant, lon_low, lon_high, lat_low, lat_high)


def neighbours(axis, periodic):
    count = lax.axis_size(axis)
    forward = [(i, i + 1) for i in range(count - 1)]
    if periodic:
        forward.append((count - 1, 0))
    backward = [(target, source) for source, target in forward]
    return forward, backward


def on_device(trajectory, cotangent, courant, branch, cloud_list, cloud_count):
    fields, nlon, nlat, lev = cotangent.shape
    cloudy = cloudy_columns(cloud_list, cloud_count, nlon * nlat)
    mask = jnp.broadcast_to(cloudy.reshape(nlon, nlat, 1), (nlon, nlat, lev)).astype(jnp.float32)
    first = first_pair(trajectory, cotangent, branch, mask)
    after = lambda dim, start: jnp.concatenate(
        [lax.slice_in_dim(first, start, start + 2, axis=dim), lax.slice_in_dim(cotangent[2:], start, start + 2, axis=dim)], 0
    )
    weight = lambda dim, start: lax.slice_in_dim(courant[dim - 1], start, start + 2, axis=dim - 1)
    forward, backward = neighbours("lon", True)
    lon_low = lax.ppermute(weight(1, nlon - 2) * after(1, nlon - 2), "lon", forward)
    lon_high = lax.ppermute(weight(1, 0) * after(1, 0), "lon", backward)
    forward, backward = neighbours("lat", False)
    flat = lambda a: a.reshape(fields, 2 * nlon, lev)
    lat_low = lax.ppermute(flat(weight(2, nlat - 2) * after(2, nlat - 2)), "lat", forward)
    lat_high = lax.ppermute(flat(weight(2, 0) * after(2, 0)), "lat", backward)
    return advect(first, cotangent, courant, lon_low, lon_high, lat_low, lat_high)


def solution(mesh):
    placed = (
        P(None, "lon", "lat", None),
        P(None, "lon", "lat", None),
        P(None, "lon", "lat", None),
        P("lon", "lat", None),
        P("lon", "lat", None),
        P("lon", "lat"),
    )
    return jax.shard_map(
        on_device,
        mesh=mesh,
        in_specs=placed,
        out_specs=P(None, "lon", "lat", None),
        check_vma=False,
    )
```

```python
import jax
import jax.numpy as jnp
from jax import lax
from jax.experimental import pallas as pl
from jax.experimental.pallas import tpu as pltpu
from jax.sharding import PartitionSpec as P

NEWT = 4


growth = 0.5
latent_liquid = 1.0
latent_ice = 1.3


def increments(warmth, vapour, kinds):
    mixed = jax.nn.sigmoid(2.0 * warmth)
    liquid_share = jnp.where(kinds == 1, 1.0, jnp.where(kinds == 2, 0.0, mixed))
    latent = latent_liquid * liquid_share + latent_ice * (1.0 - liquid_share)
    active = (kinds > 0).astype(warmth.dtype)
    amount = jnp.zeros_like(warmth)
    for newton_step in range(NEWT):
        saturated = jnp.exp(growth * (warmth + latent * amount))
        excess = vapour - amount - saturated
        amount = amount + excess / (1.0 + growth * latent * saturated)
    amount = active * amount
    return (latent * amount, -amount, liquid_share * amount, (1.0 - liquid_share) * amount)


def sat_adjoint(warmth, vapour, kinds, cot_heat, cot_vapour, cot_liquid, cot_ice):

    def forward(first_in, second_in):
        return increments(first_in, second_in, kinds)

    unused, pullback = jax.vjp(forward, warmth, vapour)
    grad_heat, grad_vapour = pullback((cot_heat, cot_vapour, cot_liquid, cot_ice))
    return (cot_heat + grad_heat, cot_vapour + grad_vapour)


def cloudy_columns(cloud_list, cloud_count, columns):
    index = cloud_list[0, 0]
    count = cloud_count[0, 0]
    slot = jnp.arange(index.shape[0], dtype=jnp.int32)
    hit = (index[:, None] == jnp.arange(columns, dtype=jnp.int32)[None, :]) & (slot < count)[:, None]
    return jnp.any(hit, axis=0)


def sat_kernel(traj_ref, cot_ref, kind_ref, mask_ref, out_ref):
    rows, nlat = traj_ref.shape[1], traj_ref.shape[2]
    chunk = 32
    for i in range(rows * (nlat // chunk)):
        r = i // (nlat // chunk)
        lat = pl.ds((i % (nlat // chunk)) * chunk, chunk)
        cot = [cot_ref[k, r, lat, :] for k in range(4)]
        new_heat, new_vapour = sat_adjoint(
            traj_ref[0, r, lat, :], traj_ref[1, r, lat, :], kind_ref[r, lat, :], *cot
        )
        cloudy = mask_ref[r, lat, :] > 0.0
        out_ref[0, r, lat, :] = jnp.where(cloudy, new_heat, cot[0])
        out_ref[1, r, lat, :] = jnp.where(cloudy, new_vapour, cot[1])


def first_pair(trajectory, cotangent, branch, mask):
    _, nlon, nlat, lev = trajectory.shape
    rows = 8
    return pl.pallas_call(
        sat_kernel,
        grid=(nlon // rows,),
        in_specs=[
            pl.BlockSpec((2, rows, nlat, lev), lambda i: (0, i, 0, 0)),
            pl.BlockSpec((4, rows, nlat, lev), lambda i: (0, i, 0, 0)),
            pl.BlockSpec((rows, nlat, lev), lambda i: (i, 0, 0)),
            pl.BlockSpec((rows, nlat, lev), lambda i: (i, 0, 0)),
        ],
        out_specs=pl.BlockSpec((2, rows, nlat, lev), lambda i: (0, i, 0, 0)),
        out_shape=jax.ShapeDtypeStruct((2, nlon, nlat, lev), jnp.float32),
    )(trajectory, cotangent, branch, mask)


def stencil_kernel(first_ref, cot_ref, cour_ref, out_ref, lon_pad, lat_pad):
    nlon, nlat = out_ref.shape[1], out_ref.shape[2]
    f = pl.program_id(0)
    zeros = jnp.zeros((2,) + lon_pad.shape[1:], jnp.float32)

    def compute(src):
        for r in range(nlon):
            lon_pad[r + 2] = cour_ref[0, r] * src[0, r]
        lon_pad[0:2] = zeros
        lon_pad[nlon + 2:nlon + 4] = zeros
        lat_pad[6:8] = zeros[0, 0:2]
        lat_pad[8 + nlat:10 + nlat] = zeros[0, 0:2]
        for r in range(nlon):
            lat_pad[8:8 + nlat] = cour_ref[1, r] * src[0, r]
            d_lat = (8.0 * (lat_pad[9:9 + nlat] - lat_pad[7:7 + nlat]) - (lat_pad[10:10 + nlat] - lat_pad[6:6 + nlat])) / 12.0
            d_lon = (8.0 * (lon_pad[r + 3] - lon_pad[r + 1]) - (lon_pad[r + 4] - lon_pad[r])) / 12.0
            out_ref[0, r] = src[0, r] + d_lon + d_lat

    @pl.when(f < 2)
    def _():
        compute(first_ref)

    @pl.when(f >= 2)
    def _():
        compute(cot_ref)


def advect(first, cotangent, courant):
    fields, nlon, nlat, lev = cotangent.shape
    size = cotangent.size * 4
    return pl.pallas_call(
        stencil_kernel,
        grid=(fields,),
        in_specs=[
            pl.BlockSpec((1, nlon, nlat, lev), lambda f: (jnp.minimum(f, 1), 0, 0, 0)),
            pl.BlockSpec((1, nlon, nlat, lev), lambda f: (f, 0, 0, 0)),
            pl.BlockSpec((2, nlon, nlat, lev), lambda f: (0, 0, 0, 0)),
        ],
        out_specs=pl.BlockSpec((1, nlon, nlat, lev), lambda f: (f, 0, 0, 0)),
        out_shape=jax.ShapeDtypeStruct(cotangent.shape, jnp.float32),
        scratch_shapes=[
            pltpu.VMEM((nlon + 4, nlat, lev), jnp.float32),
            pltpu.VMEM((nlat + 16, lev), jnp.float32),
        ],
        cost_estimate=pl.CostEstimate(flops=12 * cotangent.size, transcendentals=0, bytes_accessed=3 * size),
    )(first, cotangent, courant)


def halo_kernel(lon_low, lon_high, lat_low, lat_high, out_hbm, out_ref, lon_lo_buf, lon_hi_buf, lat_lo_buf, lat_hi_buf, sems):
    fields, nlon, nlat, lev = out_hbm.shape
    regions = [
        (out_hbm.at[:, 0:2], lon_lo_buf),
        (out_hbm.at[:, nlon - 2:nlon], lon_hi_buf),
        (out_hbm.at[:, 2:nlon - 2, 0:8], lat_lo_buf),
        (out_hbm.at[:, 2:nlon - 2, nlat - 8:nlat], lat_hi_buf),
    ]
    copies = [pltpu.make_async_copy(src, dst, sems.at[i]) for i, (src, dst) in enumerate(regions)]
    for c in copies:
        c.start()
    for c in copies:
        c.wait()
    lane = lax.broadcasted_iota(jnp.int32, (8, lev), 0)

    def lat_fix(tile, low_rows, high_rows, at_low):
        if at_low:
            row0 = (low_rows[0:1] - 8.0 * low_rows[1:2]) / 12.0
            row1 = low_rows[1:2] / 12.0
            return tile + jnp.where(lane == 0, row0, jnp.where(lane == 1, row1, 0.0))
        row6 = -high_rows[0:1] / 12.0
        row7 = (8.0 * high_rows[0:1] - high_rows[1:2]) / 12.0
        return tile + jnp.where(lane == 6, row6, jnp.where(lane == 7, row7, 0.0))

    for f in range(fields):
        lo = lon_low[f]
        hi = lon_high[f]
        first = [(lo[0] - 8.0 * lo[1]) / 12.0, lo[1] / 12.0]
        last = [-hi[0] / 12.0, (8.0 * hi[0] - hi[1]) / 12.0]
        for k, r in enumerate((0, 1)):
            block = lon_lo_buf[f, k] + first[k]
            low_rows = lat_low[f, 2 * r:2 * r + 2]
            high_rows = lat_high[f, 2 * r:2 * r + 2]
            lon_lo_buf[f, k] = block
            lon_lo_buf[f, k, 0:8] = lat_fix(block[0:8], low_rows, high_rows, True)
            lon_lo_buf[f, k, nlat - 8:nlat] = lat_fix(block[nlat - 8:nlat], low_rows, high_rows, False)
        for k, r in enumerate((nlon - 2, nlon - 1)):
            block = lon_hi_buf[f, k] + last[k]
            low_rows = lat_low[f, 2 * r:2 * r + 2]
            high_rows = lat_high[f, 2 * r:2 * r + 2]
            lon_hi_buf[f, k] = block
            lon_hi_buf[f, k, 0:8] = lat_fix(block[0:8], low_rows, high_rows, True)
            lon_hi_buf[f, k, nlat - 8:nlat] = lat_fix(block[nlat - 8:nlat], low_rows, high_rows, False)
        for r in range(2, nlon - 2):
            low_rows = lat_low[f, 2 * r:2 * r + 2]
            high_rows = lat_high[f, 2 * r:2 * r + 2]
            lat_lo_buf[f, r - 2] = lat_fix(lat_lo_buf[f, r - 2], low_rows, high_rows, True)
            lat_hi_buf[f, r - 2] = lat_fix(lat_hi_buf[f, r - 2], low_rows, high_rows, False)
    copies = [pltpu.make_async_copy(dst, src, sems.at[i]) for i, (src, dst) in enumerate(regions)]
    for c in copies:
        c.start()
    for c in copies:
        c.wait()


def add_halos(out, lon_low, lon_high, lat_low, lat_high):
    fields, nlon, nlat, lev = out.shape
    vmem = pl.BlockSpec(memory_space=pltpu.VMEM)
    return pl.pallas_call(
        halo_kernel,
        in_specs=[vmem, vmem, vmem, vmem, pl.BlockSpec(memory_space=pl.ANY)],
        out_specs=pl.BlockSpec(memory_space=pl.ANY),
        out_shape=jax.ShapeDtypeStruct(out.shape, jnp.float32),
        scratch_shapes=[
            pltpu.VMEM((fields, 2, nlat, lev), jnp.float32),
            pltpu.VMEM((fields, 2, nlat, lev), jnp.float32),
            pltpu.VMEM((fields, nlon - 4, 8, lev), jnp.float32),
            pltpu.VMEM((fields, nlon - 4, 8, lev), jnp.float32),
            pltpu.SemaphoreType.DMA((4,)),
        ],
        input_output_aliases={4: 0},
    )(lon_low, lon_high, lat_low, lat_high, out)


def neighbours(axis, periodic):
    count = lax.axis_size(axis)
    forward = [(i, i + 1) for i in range(count - 1)]
    if periodic:
        forward.append((count - 1, 0))
    backward = [(target, source) for source, target in forward]
    return forward, backward


def on_device(trajectory, cotangent, courant, branch, cloud_list, cloud_count):
    fields, nlon, nlat, lev = cotangent.shape
    cloudy = cloudy_columns(cloud_list, cloud_count, nlon * nlat)
    mask = jnp.broadcast_to(cloudy.reshape(nlon, nlat, 1), (nlon, nlat, lev)).astype(jnp.float32)
    first = first_pair(trajectory, cotangent, branch, mask)
    after = lambda dim, start: jnp.concatenate(
        [lax.slice_in_dim(first, start, start + 2, axis=dim), lax.slice_in_dim(cotangent[2:], start, start + 2, axis=dim)], 0
    )
    weight = lambda dim, start: lax.slice_in_dim(courant[dim - 1], start, start + 2, axis=dim - 1)
    forward, backward = neighbours("lon", True)
    lon_low = lax.ppermute(weight(1, nlon - 2) * after(1, nlon - 2), "lon", forward)
    lon_high = lax.ppermute(weight(1, 0) * after(1, 0), "lon", backward)
    forward, backward = neighbours("lat", False)
    flat = lambda a: a.reshape(fields, 2 * nlon, lev)
    lat_low = lax.ppermute(flat(weight(2, nlat - 2) * after(2, nlat - 2)), "lat", forward)
    lat_high = lax.ppermute(flat(weight(2, 0) * after(2, 0)), "lat", backward)
    out = advect(first, cotangent, courant)
    return add_halos(out, lon_low, lon_high, lat_low, lat_high)


def solution(mesh):
    placed = (
        P(None, "lon", "lat", None),
        P(None, "lon", "lat", None),
        P(None, "lon", "lat", None),
        P("lon", "lat", None),
        P("lon", "lat", None),
        P("lon", "lat"),
    )
    return jax.shard_map(
        on_device,
        mesh=mesh,
        in_specs=placed,
        out_specs=P(None, "lon", "lat", None),
        check_vma=False,
    )
```

```python
import jax
import jax.numpy as jnp
from jax import lax
from jax.experimental import pallas as pl
from jax.experimental.pallas import tpu as pltpu
from jax.sharding import PartitionSpec as P

NEWT = 4


growth = 0.5
latent_liquid = 1.0
latent_ice = 1.3


def increments(warmth, vapour, kinds):
    mixed = jax.nn.sigmoid(2.0 * warmth)
    liquid_share = jnp.where(kinds == 1, 1.0, jnp.where(kinds == 2, 0.0, mixed))
    latent = latent_liquid * liquid_share + latent_ice * (1.0 - liquid_share)
    active = (kinds > 0).astype(warmth.dtype)
    amount = jnp.zeros_like(warmth)
    for newton_step in range(NEWT):
        saturated = jnp.exp(growth * (warmth + latent * amount))
        excess = vapour - amount - saturated
        amount = amount + excess / (1.0 + growth * latent * saturated)
    amount = active * amount
    return (latent * amount, -amount, liquid_share * amount, (1.0 - liquid_share) * amount)


def sat_adjoint(warmth, vapour, kinds, cot_heat, cot_vapour, cot_liquid, cot_ice):

    def forward(first_in, second_in):
        return increments(first_in, second_in, kinds)

    unused, pullback = jax.vjp(forward, warmth, vapour)
    grad_heat, grad_vapour = pullback((cot_heat, cot_vapour, cot_liquid, cot_ice))
    return (cot_heat + grad_heat, cot_vapour + grad_vapour)


def cloudy_columns(cloud_list, cloud_count, nlon, nlat, rows):
    index = cloud_list[0, 0]
    count = cloud_count[0, 0]
    slot = jnp.arange(index.shape[0], dtype=jnp.int32)
    lon = jnp.arange(nlon, dtype=jnp.int32).reshape(nlon // rows, 1, rows)
    lat = jnp.arange(nlat, dtype=jnp.int32).reshape(1, nlat, 1)
    column = (lon * nlat + lat)[None]
    hit = (index[:, None, None, None] == column) & (slot < count)[:, None, None, None]
    return jnp.any(hit, axis=0).astype(jnp.float32)


def sat_kernel(traj_ref, cot_ref, kind_ref, mask_ref, cour_ref,
               out_ref, lon_bottom, lon_top, lat_bottom, lat_top):
    fields, rows, nlat, lev = cot_ref.shape
    step = pl.program_id(0)
    last = pl.num_programs(0) - 1
    chunk = 32
    parts = nlat // chunk
    for r in range(rows):
        after = [[None] * parts for _ in range(fields)]
        for j in range(parts):
            lat = pl.ds(j * chunk, chunk)
            cot = [cot_ref[k, r, lat, :] for k in range(4)]
            new_heat, new_vapour = sat_adjoint(
                traj_ref[0, r, lat, :], traj_ref[1, r, lat, :], kind_ref[r, lat, :], *cot
            )
            cloudy = jnp.broadcast_to(mask_ref[0, lat, r:r + 1], (chunk, lev)) > 0.0
            heat = jnp.where(cloudy, new_heat, cot[0])
            vapour = jnp.where(cloudy, new_vapour, cot[1])
            out_ref[0, r, lat, :] = heat
            out_ref[1, r, lat, :] = vapour
            after[0][j] = heat
            after[1][j] = vapour
            for f in range(2, fields):
                after[f][j] = cot_ref[f, r, lat, :]
        low_weight = cour_ref[1, r, 0:2, :]
        high_weight = cour_ref[1, r, nlat - 2:nlat, :]
        for f in range(fields):
            lat_bottom[f, 2 * r:2 * r + 2, :] = low_weight * after[f][0][0:2]
            lat_top[f, 2 * r:2 * r + 2, :] = high_weight * after[f][parts - 1][chunk - 2:chunk]
        if r < 2:
            @pl.when(step == 0)
            def _():
                for f in range(fields):
                    for j in range(parts):
                        lat = pl.ds(j * chunk, chunk)
                        lon_bottom[f, r, lat, :] = cour_ref[0, r, lat, :] * after[f][j]
        if r >= rows - 2:
            @pl.when(step == last)
            def _():
                for f in range(fields):
                    for j in range(parts):
                        lat = pl.ds(j * chunk, chunk)
                        lon_top[f, r - rows + 2, lat, :] = cour_ref[0, r, lat, :] * after[f][j]


def first_pair(trajectory, cotangent, branch, mask, courant, rows):
    fields, nlon, nlat, lev = cotangent.shape
    lon_send = jax.ShapeDtypeStruct((fields, 2, nlat, lev), jnp.float32)
    lat_send = jax.ShapeDtypeStruct((fields, 2 * nlon, lev), jnp.float32)
    return pl.pallas_call(
        sat_kernel,
        grid=(nlon // rows,),
        in_specs=[
            pl.BlockSpec((2, rows, nlat, lev), lambda i: (0, i, 0, 0)),
            pl.BlockSpec((fields, rows, nlat, lev), lambda i: (0, i, 0, 0)),
            pl.BlockSpec((rows, nlat, lev), lambda i: (i, 0, 0)),
            pl.BlockSpec((1, nlat, rows), lambda i: (i, 0, 0)),
            pl.BlockSpec((2, rows, nlat, lev), lambda i: (0, i, 0, 0)),
        ],
        out_specs=[
            pl.BlockSpec((2, rows, nlat, lev), lambda i: (0, i, 0, 0)),
            pl.BlockSpec((fields, 2, nlat, lev), lambda i: (0, 0, 0, 0)),
            pl.BlockSpec((fields, 2, nlat, lev), lambda i: (0, 0, 0, 0)),
            pl.BlockSpec((fields, 2 * rows, lev), lambda i: (0, i, 0)),
            pl.BlockSpec((fields, 2 * rows, lev), lambda i: (0, i, 0)),
        ],
        out_shape=[jax.ShapeDtypeStruct((2, nlon, nlat, lev), jnp.float32), lon_send, lon_send, lat_send, lat_send],
    )(trajectory, cotangent, branch, mask, courant)


def stencil_kernel(first_ref, cot_ref, cour_ref, out_ref, lon_pad, lat_pad):
    nlon, nlat = out_ref.shape[1], out_ref.shape[2]
    f = pl.program_id(0)
    zeros = jnp.zeros((2,) + lon_pad.shape[1:], jnp.float32)

    def compute(src):
        for r in range(nlon):
            lon_pad[r + 2] = cour_ref[0, r] * src[0, r]
        lon_pad[0:2] = zeros
        lon_pad[nlon + 2:nlon + 4] = zeros
        lat_pad[6:8] = zeros[0, 0:2]
        lat_pad[8 + nlat:10 + nlat] = zeros[0, 0:2]
        for r in range(nlon):
            lat_pad[8:8 + nlat] = cour_ref[1, r] * src[0, r]
            d_lat = (8.0 * (lat_pad[9:9 + nlat] - lat_pad[7:7 + nlat]) - (lat_pad[10:10 + nlat] - lat_pad[6:6 + nlat])) / 12.0
            d_lon = (8.0 * (lon_pad[r + 3] - lon_pad[r + 1]) - (lon_pad[r + 4] - lon_pad[r])) / 12.0
            out_ref[0, r] = src[0, r] + d_lon + d_lat

    @pl.when(f < 2)
    def _():
        compute(first_ref)

    @pl.when(f >= 2)
    def _():
        compute(cot_ref)


def advect(first, cotangent, courant):
    fields, nlon, nlat, lev = cotangent.shape
    size = cotangent.size * 4
    return pl.pallas_call(
        stencil_kernel,
        grid=(fields,),
        in_specs=[
            pl.BlockSpec((1, nlon, nlat, lev), lambda f: (jnp.minimum(f, 1), 0, 0, 0)),
            pl.BlockSpec((1, nlon, nlat, lev), lambda f: (f, 0, 0, 0)),
            pl.BlockSpec((2, nlon, nlat, lev), lambda f: (0, 0, 0, 0)),
        ],
        out_specs=pl.BlockSpec((1, nlon, nlat, lev), lambda f: (f, 0, 0, 0)),
        out_shape=jax.ShapeDtypeStruct(cotangent.shape, jnp.float32),
        scratch_shapes=[
            pltpu.VMEM((nlon + 4, nlat, lev), jnp.float32),
            pltpu.VMEM((nlat + 16, lev), jnp.float32),
        ],
        cost_estimate=pl.CostEstimate(flops=12 * cotangent.size, transcendentals=0, bytes_accessed=3 * size),
    )(first, cotangent, courant)


def halo_kernel(lon_low_hbm, lon_high_hbm, lat_low_hbm, lat_high_hbm, out_hbm, out_ref,
                lon_low, lon_high, lat_low, lat_high, lon_lo_buf, lon_hi_buf, lat_lo_buf, lat_hi_buf, sems):
    fields, nlon, nlat, lev = out_hbm.shape
    halos = [(lon_low_hbm, lon_low), (lon_high_hbm, lon_high), (lat_low_hbm, lat_low), (lat_high_hbm, lat_high)]
    regions = [
        (out_hbm.at[:, 0:2], lon_lo_buf),
        (out_hbm.at[:, nlon - 2:nlon], lon_hi_buf),
        (out_hbm.at[:, 2:nlon - 2, 0:8], lat_lo_buf),
        (out_hbm.at[:, 2:nlon - 2, nlat - 8:nlat], lat_hi_buf),
    ]
    copies = [pltpu.make_async_copy(s, d, sems.at[i]) for i, (s, d) in enumerate(halos + regions)]
    for c in copies:
        c.start()
    for c in copies:
        c.wait()
    sub = lax.broadcasted_iota(jnp.int32, (8, lev), 0)

    def lat_fix(tile, low_rows, high_rows, at_low):
        if at_low:
            row0 = (low_rows[0:1] - 8.0 * low_rows[1:2]) / 12.0
            row1 = low_rows[1:2] / 12.0
            return tile + jnp.where(sub == 0, row0, jnp.where(sub == 1, row1, 0.0))
        row6 = -high_rows[0:1] / 12.0
        row7 = (8.0 * high_rows[0:1] - high_rows[1:2]) / 12.0
        return tile + jnp.where(sub == 6, row6, jnp.where(sub == 7, row7, 0.0))

    for f in range(fields):
        lo = lon_low[f]
        hi = lon_high[f]
        edge_terms = [(lo[0] - 8.0 * lo[1]) / 12.0, lo[1] / 12.0, -hi[0] / 12.0, (8.0 * hi[0] - hi[1]) / 12.0]
        for k, r in enumerate((0, 1, nlon - 2, nlon - 1)):
            buf = lon_lo_buf if k < 2 else lon_hi_buf
            block = buf[f, k % 2] + edge_terms[k]
            low_rows = lat_low[f, 2 * r:2 * r + 2]
            high_rows = lat_high[f, 2 * r:2 * r + 2]
            buf[f, k % 2] = block
            buf[f, k % 2, 0:8] = lat_fix(block[0:8], low_rows, high_rows, True)
            buf[f, k % 2, nlat - 8:nlat] = lat_fix(block[nlat - 8:nlat], low_rows, high_rows, False)
        for r in range(2, nlon - 2):
            low_rows = lat_low[f, 2 * r:2 * r + 2]
            high_rows = lat_high[f, 2 * r:2 * r + 2]
            lat_lo_buf[f, r - 2] = lat_fix(lat_lo_buf[f, r - 2], low_rows, high_rows, True)
            lat_hi_buf[f, r - 2] = lat_fix(lat_hi_buf[f, r - 2], low_rows, high_rows, False)
    copies = [pltpu.make_async_copy(d, s, sems.at[4 + i]) for i, (s, d) in enumerate(regions)]
    for c in copies:
        c.start()
    for c in copies:
        c.wait()


def add_halos(out, lon_low, lon_high, lat_low, lat_high):
    fields, nlon, nlat, lev = out.shape
    hbm = pl.BlockSpec(memory_space=pl.ANY)
    return pl.pallas_call(
        halo_kernel,
        in_specs=[hbm] * 5,
        out_specs=hbm,
        out_shape=jax.ShapeDtypeStruct(out.shape, jnp.float32),
        scratch_shapes=[
            pltpu.VMEM(lon_low.shape, jnp.float32),
            pltpu.VMEM(lon_high.shape, jnp.float32),
            pltpu.VMEM(lat_low.shape, jnp.float32),
            pltpu.VMEM(lat_high.shape, jnp.float32),
            pltpu.VMEM((fields, 2, nlat, lev), jnp.float32),
            pltpu.VMEM((fields, 2, nlat, lev), jnp.float32),
            pltpu.VMEM((fields, nlon - 4, 8, lev), jnp.float32),
            pltpu.VMEM((fields, nlon - 4, 8, lev), jnp.float32),
            pltpu.SemaphoreType.DMA((8,)),
        ],
        input_output_aliases={4: 0},
    )(lon_low, lon_high, lat_low, lat_high, out)


def neighbours(axis, periodic):
    count = lax.axis_size(axis)
    forward = [(i, i + 1) for i in range(count - 1)]
    if periodic:
        forward.append((count - 1, 0))
    backward = [(target, source) for source, target in forward]
    return forward, backward


def on_device(trajectory, cotangent, courant, branch, cloud_list, cloud_count):
    fields, nlon, nlat, lev = cotangent.shape
    rows = 8
    mask = cloudy_columns(cloud_list, cloud_count, nlon, nlat, rows)
    first, lon_bottom, lon_top, lat_bottom, lat_top = first_pair(trajectory, cotangent, branch, mask, courant, rows)
    forward, backward = neighbours("lon", True)
    lon_low = lax.ppermute(lon_top, "lon", forward)
    lon_high = lax.ppermute(lon_bottom, "lon", backward)
    forward, backward = neighbours("lat", False)
    lat_low = lax.ppermute(lat_top, "lat", forward)
    lat_high = lax.ppermute(lat_bottom, "lat", backward)
    out = advect(first, cotangent, courant)
    return add_halos(out, lon_low, lon_high, lat_low, lat_high)


def solution(mesh):
    placed = (
        P(None, "lon", "lat", None),
        P(None, "lon", "lat", None),
        P(None, "lon", "lat", None),
        P("lon", "lat", None),
        P("lon", "lat", None),
        P("lon", "lat"),
    )
    return jax.shard_map(
        on_device,
        mesh=mesh,
        in_specs=placed,
        out_specs=P(None, "lon", "lat", None),
        check_vma=False,
    )
```

```python
import jax
import jax.numpy as jnp
from jax import lax
from jax.experimental import pallas as pl
from jax.experimental.pallas import tpu as pltpu
from jax.sharding import PartitionSpec as P

NEWT = 4


growth = 0.5
latent_liquid = 1.0
latent_ice = 1.3


def increments(warmth, vapour, kinds):
    mixed = jax.nn.sigmoid(2.0 * warmth)
    liquid_share = jnp.where(kinds == 1, 1.0, jnp.where(kinds == 2, 0.0, mixed))
    latent = latent_liquid * liquid_share + latent_ice * (1.0 - liquid_share)
    active = (kinds > 0).astype(warmth.dtype)
    amount = jnp.zeros_like(warmth)
    for newton_step in range(NEWT):
        saturated = jnp.exp(growth * (warmth + latent * amount))
        excess = vapour - amount - saturated
        amount = amount + excess / (1.0 + growth * latent * saturated)
    amount = active * amount
    return (latent * amount, -amount, liquid_share * amount, (1.0 - liquid_share) * amount)


def sat_adjoint(warmth, vapour, kinds, cot_heat, cot_vapour, cot_liquid, cot_ice):

    def forward(first_in, second_in):
        return increments(first_in, second_in, kinds)

    unused, pullback = jax.vjp(forward, warmth, vapour)
    grad_heat, grad_vapour = pullback((cot_heat, cot_vapour, cot_liquid, cot_ice))
    return (cot_heat + grad_heat, cot_vapour + grad_vapour)


def cloudy_columns(cloud_list, cloud_count, nlon, nlat, rows):
    index = cloud_list[0, 0]
    count = cloud_count[0, 0]
    slot = jnp.arange(index.shape[0], dtype=jnp.int32)
    hit = (index[:, None] == jnp.arange(nlon * nlat, dtype=jnp.int32)[None, :]) & (slot < count)[:, None]
    cloudy = jnp.any(hit, axis=0).astype(jnp.float32)
    return jnp.transpose(cloudy.reshape(nlon // rows, rows, nlat), (0, 2, 1))


def sat_kernel(traj_ref, cot_ref, kind_ref, mask_ref, cour_ref,
               out_ref, lon_bottom, lon_top, lat_bottom, lat_top):
    fields, rows, nlat, lev = cot_ref.shape
    step = pl.program_id(0)
    last = pl.num_programs(0) - 1
    chunk = 32
    parts = nlat // chunk
    for r in range(rows):
        after = [[None] * parts for _ in range(fields)]
        for j in range(parts):
            lat = pl.ds(j * chunk, chunk)
            cot = [cot_ref[k, r, lat, :] for k in range(4)]
            new_heat, new_vapour = sat_adjoint(
                traj_ref[0, r, lat, :], traj_ref[1, r, lat, :], kind_ref[r, lat, :], *cot
            )
            cloudy = jnp.broadcast_to(mask_ref[0, lat, r:r + 1], (chunk, lev)) > 0.0
            heat = jnp.where(cloudy, new_heat, cot[0])
            vapour = jnp.where(cloudy, new_vapour, cot[1])
            out_ref[0, r, lat, :] = heat
            out_ref[1, r, lat, :] = vapour
            after[0][j] = heat
            after[1][j] = vapour
            for f in range(2, fields):
                after[f][j] = cot_ref[f, r, lat, :]
        low_weight = cour_ref[1, r, 0:2, :]
        high_weight = cour_ref[1, r, nlat - 2:nlat, :]
        for f in range(fields):
            lat_bottom[f, 2 * r:2 * r + 2, :] = low_weight * after[f][0][0:2]
            lat_top[f, 2 * r:2 * r + 2, :] = high_weight * after[f][parts - 1][chunk - 2:chunk]
        if r < 2:
            @pl.when(step == 0)
            def _():
                for f in range(fields):
                    for j in range(parts):
                        lat = pl.ds(j * chunk, chunk)
                        lon_bottom[f, r, lat, :] = cour_ref[0, r, lat, :] * after[f][j]
        if r >= rows - 2:
            @pl.when(step == last)
            def _():
                for f in range(fields):
                    for j in range(parts):
                        lat = pl.ds(j * chunk, chunk)
                        lon_top[f, r - rows + 2, lat, :] = cour_ref[0, r, lat, :] * after[f][j]


def first_pair(trajectory, cotangent, branch, mask, courant, rows):
    fields, nlon, nlat, lev = cotangent.shape
    lon_send = jax.ShapeDtypeStruct((fields, 2, nlat, lev), jnp.float32)
    lat_send = jax.ShapeDtypeStruct((fields, 2 * nlon, lev), jnp.float32)
    return pl.pallas_call(
        sat_kernel,
        grid=(nlon // rows,),
        in_specs=[
            pl.BlockSpec((2, rows, nlat, lev), lambda i: (0, i, 0, 0)),
            pl.BlockSpec((fields, rows, nlat, lev), lambda i: (0, i, 0, 0)),
            pl.BlockSpec((rows, nlat, lev), lambda i: (i, 0, 0)),
            pl.BlockSpec((1, nlat, rows), lambda i: (i, 0, 0)),
            pl.BlockSpec((2, rows, nlat, lev), lambda i: (0, i, 0, 0)),
        ],
        out_specs=[
            pl.BlockSpec((2, rows, nlat, lev), lambda i: (0, i, 0, 0)),
            pl.BlockSpec((fields, 2, nlat, lev), lambda i: (0, 0, 0, 0)),
            pl.BlockSpec((fields, 2, nlat, lev), lambda i: (0, 0, 0, 0)),
            pl.BlockSpec((fields, 2 * rows, lev), lambda i: (0, i, 0)),
            pl.BlockSpec((fields, 2 * rows, lev), lambda i: (0, i, 0)),
        ],
        out_shape=[jax.ShapeDtypeStruct((2, nlon, nlat, lev), jnp.float32), lon_send, lon_send, lat_send, lat_send],
    )(trajectory, cotangent, branch, mask, courant)


def stencil_kernel(first_hbm, cot_hbm, cour_hbm, out_hbm, field_v, cour_v, out_v, lon_pad, lat_pad, in_sems, out_sems):
    fields, nlon, nlat, lev = cot_hbm.shape
    zeros = jnp.zeros((2, nlat, lev), jnp.float32)
    cour_copy = pltpu.make_async_copy(cour_hbm, cour_v, in_sems.at[0])
    cour_copy.start()
    loads = [pltpu.make_async_copy(first_hbm, field_v.at[0:2], in_sems.at[1])]
    loads += [pltpu.make_async_copy(cot_hbm.at[f], field_v.at[f], in_sems.at[f]) for f in range(2, fields)]
    for c in loads:
        c.start()
    lon_pad[0:2] = zeros
    lon_pad[nlon + 2:nlon + 4] = zeros
    lat_pad[6:8] = zeros[0, 0:2]
    lat_pad[8 + nlat:10 + nlat] = zeros[0, 0:2]
    cour_copy.wait()
    stores = []
    for f in range(fields):
        if f == 0:
            loads[0].wait()
        elif f >= 2:
            loads[f - 1].wait()
        src = field_v.at[f]
        for r in range(nlon):
            lon_pad[r + 2] = cour_v[0, r] * src[r]
        for r in range(nlon):
            lat_pad[8:8 + nlat] = cour_v[1, r] * src[r]
            d_lat = (8.0 * (lat_pad[9:9 + nlat] - lat_pad[7:7 + nlat]) - (lat_pad[10:10 + nlat] - lat_pad[6:6 + nlat])) / 12.0
            d_lon = (8.0 * (lon_pad[r + 3] - lon_pad[r + 1]) - (lon_pad[r + 4] - lon_pad[r])) / 12.0
            out_v[f, r] = src[r] + d_lon + d_lat
        store = pltpu.make_async_copy(out_v.at[f], out_hbm.at[f], out_sems.at[f])
        store.start()
        stores.append(store)
    for store in stores:
        store.wait()


def advect(first, cotangent, courant):
    fields, nlon, nlat, lev = cotangent.shape
    size = cotangent.size * 4
    hbm = pl.BlockSpec(memory_space=pl.ANY)
    return pl.pallas_call(
        stencil_kernel,
        in_specs=[hbm, hbm, hbm],
        out_specs=hbm,
        out_shape=jax.ShapeDtypeStruct(cotangent.shape, jnp.float32),
        scratch_shapes=[
            pltpu.VMEM(cotangent.shape, jnp.float32),
            pltpu.VMEM(courant.shape, jnp.float32),
            pltpu.VMEM(cotangent.shape, jnp.float32),
            pltpu.VMEM((nlon + 4, nlat, lev), jnp.float32),
            pltpu.VMEM((nlat + 16, lev), jnp.float32),
            pltpu.SemaphoreType.DMA((fields,)),
            pltpu.SemaphoreType.DMA((fields,)),
        ],
        cost_estimate=pl.CostEstimate(flops=12 * cotangent.size, transcendentals=0, bytes_accessed=3 * size),
    )(first, cotangent, courant)


def halo_kernel(lon_low_hbm, lon_high_hbm, lat_low_hbm, lat_high_hbm, out_hbm, out_ref,
                lon_low, lon_high, lat_low, lat_high, lon_lo_buf, lon_hi_buf, lat_lo_buf, lat_hi_buf, sems):
    fields, nlon, nlat, lev = out_hbm.shape
    halos = [(lon_low_hbm, lon_low), (lon_high_hbm, lon_high), (lat_low_hbm, lat_low), (lat_high_hbm, lat_high)]
    regions = [
        (out_hbm.at[:, 0:2], lon_lo_buf),
        (out_hbm.at[:, nlon - 2:nlon], lon_hi_buf),
        (out_hbm.at[:, 2:nlon - 2, 0:8], lat_lo_buf),
        (out_hbm.at[:, 2:nlon - 2, nlat - 8:nlat], lat_hi_buf),
    ]
    copies = [pltpu.make_async_copy(s, d, sems.at[i]) for i, (s, d) in enumerate(halos + regions)]
    for c in copies:
        c.start()
    for c in copies:
        c.wait()
    sub = lax.broadcasted_iota(jnp.int32, (8, lev), 0)

    def lat_fix(tile, low_rows, high_rows, at_low):
        if at_low:
            row0 = (low_rows[0:1] - 8.0 * low_rows[1:2]) / 12.0
            row1 = low_rows[1:2] / 12.0
            return tile + jnp.where(sub == 0, row0, jnp.where(sub == 1, row1, 0.0))
        row6 = -high_rows[0:1] / 12.0
        row7 = (8.0 * high_rows[0:1] - high_rows[1:2]) / 12.0
        return tile + jnp.where(sub == 6, row6, jnp.where(sub == 7, row7, 0.0))

    for f in range(fields):
        lo = lon_low[f]
        hi = lon_high[f]
        edge_terms = [(lo[0] - 8.0 * lo[1]) / 12.0, lo[1] / 12.0, -hi[0] / 12.0, (8.0 * hi[0] - hi[1]) / 12.0]
        for k, r in enumerate((0, 1, nlon - 2, nlon - 1)):
            buf = lon_lo_buf if k < 2 else lon_hi_buf
            block = buf[f, k % 2] + edge_terms[k]
            low_rows = lat_low[f, 2 * r:2 * r + 2]
            high_rows = lat_high[f, 2 * r:2 * r + 2]
            buf[f, k % 2] = block
            buf[f, k % 2, 0:8] = lat_fix(block[0:8], low_rows, high_rows, True)
            buf[f, k % 2, nlat - 8:nlat] = lat_fix(block[nlat - 8:nlat], low_rows, high_rows, False)
        for r in range(2, nlon - 2):
            low_rows = lat_low[f, 2 * r:2 * r + 2]
            high_rows = lat_high[f, 2 * r:2 * r + 2]
            lat_lo_buf[f, r - 2] = lat_fix(lat_lo_buf[f, r - 2], low_rows, high_rows, True)
            lat_hi_buf[f, r - 2] = lat_fix(lat_hi_buf[f, r - 2], low_rows, high_rows, False)
    copies = [pltpu.make_async_copy(d, s, sems.at[4 + i]) for i, (s, d) in enumerate(regions)]
    for c in copies:
        c.start()
    for c in copies:
        c.wait()


def add_halos(out, lon_low, lon_high, lat_low, lat_high):
    fields, nlon, nlat, lev = out.shape
    hbm = pl.BlockSpec(memory_space=pl.ANY)
    return pl.pallas_call(
        halo_kernel,
        in_specs=[hbm] * 5,
        out_specs=hbm,
        out_shape=jax.ShapeDtypeStruct(out.shape, jnp.float32),
        scratch_shapes=[
            pltpu.VMEM(lon_low.shape, jnp.float32),
            pltpu.VMEM(lon_high.shape, jnp.float32),
            pltpu.VMEM(lat_low.shape, jnp.float32),
            pltpu.VMEM(lat_high.shape, jnp.float32),
            pltpu.VMEM((fields, 2, nlat, lev), jnp.float32),
            pltpu.VMEM((fields, 2, nlat, lev), jnp.float32),
            pltpu.VMEM((fields, nlon - 4, 8, lev), jnp.float32),
            pltpu.VMEM((fields, nlon - 4, 8, lev), jnp.float32),
            pltpu.SemaphoreType.DMA((8,)),
        ],
        input_output_aliases={4: 0},
    )(lon_low, lon_high, lat_low, lat_high, out)


def neighbours(axis, periodic):
    count = lax.axis_size(axis)
    forward = [(i, i + 1) for i in range(count - 1)]
    if periodic:
        forward.append((count - 1, 0))
    backward = [(target, source) for source, target in forward]
    return forward, backward


def on_device(trajectory, cotangent, courant, branch, cloud_list, cloud_count):
    fields, nlon, nlat, lev = cotangent.shape
    rows = 8
    mask = cloudy_columns(cloud_list, cloud_count, nlon, nlat, rows)
    first, lon_bottom, lon_top, lat_bottom, lat_top = first_pair(trajectory, cotangent, branch, mask, courant, rows)
    forward, backward = neighbours("lon", True)
    lon_low = lax.ppermute(lon_top, "lon", forward)
    lon_high = lax.ppermute(lon_bottom, "lon", backward)
    forward, backward = neighbours("lat", False)
    lat_low = lax.ppermute(lat_top, "lat", forward)
    lat_high = lax.ppermute(lat_bottom, "lat", backward)
    out = advect(first, cotangent, courant)
    return add_halos(out, lon_low, lon_high, lat_low, lat_high)


def solution(mesh):
    placed = (
        P(None, "lon", "lat", None),
        P(None, "lon", "lat", None),
        P(None, "lon", "lat", None),
        P("lon", "lat", None),
        P("lon", "lat", None),
        P("lon", "lat"),
    )
    return jax.shard_map(
        on_device,
        mesh=mesh,
        in_specs=placed,
        out_specs=P(None, "lon", "lat", None),
        check_vma=False,
    )
```

```python
import jax
import jax.numpy as jnp
from jax import lax
from jax.experimental import pallas as pl
from jax.experimental.pallas import tpu as pltpu
from jax.sharding import PartitionSpec as P

NEWT = 4


growth = 0.5
latent_liquid = 1.0
latent_ice = 1.3


def increments(warmth, vapour, kinds):
    mixed = jax.nn.sigmoid(2.0 * warmth)
    liquid_share = jnp.where(kinds == 1, 1.0, jnp.where(kinds == 2, 0.0, mixed))
    latent = latent_liquid * liquid_share + latent_ice * (1.0 - liquid_share)
    active = (kinds > 0).astype(warmth.dtype)
    amount = jnp.zeros_like(warmth)
    for newton_step in range(NEWT):
        saturated = jnp.exp(growth * (warmth + latent * amount))
        excess = vapour - amount - saturated
        amount = amount + excess / (1.0 + growth * latent * saturated)
    amount = active * amount
    return (latent * amount, -amount, liquid_share * amount, (1.0 - liquid_share) * amount)


def sat_adjoint(warmth, vapour, kinds, cot_heat, cot_vapour, cot_liquid, cot_ice):

    def forward(first_in, second_in):
        return increments(first_in, second_in, kinds)

    unused, pullback = jax.vjp(forward, warmth, vapour)
    grad_heat, grad_vapour = pullback((cot_heat, cot_vapour, cot_liquid, cot_ice))
    return (cot_heat + grad_heat, cot_vapour + grad_vapour)


def cloudy_columns(cloud_list, cloud_count, nlon, nlat, rows):
    index = cloud_list[0, 0]
    count = cloud_count[0, 0]
    slot = jnp.arange(index.shape[0], dtype=jnp.int32)
    hit = (index[:, None] == jnp.arange(nlon * nlat, dtype=jnp.int32)[None, :]) & (slot < count)[:, None]
    cloudy = jnp.any(hit, axis=0).astype(jnp.float32)
    return jnp.transpose(cloudy.reshape(nlon // rows, rows, nlat), (0, 2, 1))


def sat_kernel(traj_hbm, cot_hbm, kind_hbm, cour_hbm, mask_ref,
               first_hbm, lon_bottom, lon_top, lat_bottom, lat_top,
               traj_v, cot_v, kind_v, cour_v, first_v, in_sems, out_sems):
    fields, nlon, nlat, lev = cot_hbm.shape
    rows = mask_ref.shape[2]
    group = 4
    chunk = 32
    parts = nlat // chunk
    groups = []
    for g in range(nlon // group):
        span = slice(g * group, (g + 1) * group)
        pairs = [(traj_hbm.at[:, span], traj_v.at[:, span]), (cot_hbm.at[:, span], cot_v.at[:, span]),
                 (kind_hbm.at[span], kind_v.at[span]), (cour_hbm.at[:, span], cour_v.at[:, span])]
        copies = [pltpu.make_async_copy(s, d, in_sems.at[4 * g + k]) for k, (s, d) in enumerate(pairs)]
        for c in copies:
            c.start()
        groups.append(copies)
    stores = []
    for g in range(nlon // group):
        for c in groups[g]:
            c.wait()
        for r in range(g * group, (g + 1) * group):
            after = [[None] * parts for _ in range(fields)]
            for j in range(parts):
                lat = pl.ds(j * chunk, chunk)
                cot = [cot_v[k, r, lat, :] for k in range(4)]
                new_heat, new_vapour = sat_adjoint(
                    traj_v[0, r, lat, :], traj_v[1, r, lat, :], kind_v[r, lat, :], *cot
                )
                cloudy = jnp.broadcast_to(mask_ref[r // rows, lat, r % rows:r % rows + 1], (chunk, lev)) > 0.0
                heat = jnp.where(cloudy, new_heat, cot[0])
                vapour = jnp.where(cloudy, new_vapour, cot[1])
                first_v[0, r, lat, :] = heat
                first_v[1, r, lat, :] = vapour
                after[0][j] = heat
                after[1][j] = vapour
                for f in range(2, fields):
                    after[f][j] = cot_v[f, r, lat, :]
            low_weight = cour_v[1, r, 0:2, :]
            high_weight = cour_v[1, r, nlat - 2:nlat, :]
            for f in range(fields):
                lat_bottom[f, 2 * r:2 * r + 2, :] = low_weight * after[f][0][0:2]
                lat_top[f, 2 * r:2 * r + 2, :] = high_weight * after[f][parts - 1][chunk - 2:chunk]
            if r < 2 or r >= nlon - 2:
                target, at = (lon_bottom, r) if r < 2 else (lon_top, r - nlon + 2)
                for f in range(fields):
                    for j in range(parts):
                        lat = pl.ds(j * chunk, chunk)
                        target[f, at, lat, :] = cour_v[0, r, lat, :] * after[f][j]
        span = slice(g * group, (g + 1) * group)
        store = pltpu.make_async_copy(first_v.at[:, span], first_hbm.at[:, span], out_sems.at[g])
        store.start()
        stores.append(store)
    for store in stores:
        store.wait()


def first_pair(trajectory, cotangent, branch, mask, courant, rows):
    fields, nlon, nlat, lev = cotangent.shape
    lon_send = jax.ShapeDtypeStruct((fields, 2, nlat, lev), jnp.float32)
    lat_send = jax.ShapeDtypeStruct((fields, 2 * nlon, lev), jnp.float32)
    hbm = pl.BlockSpec(memory_space=pltpu.HBM)
    vmem = pl.BlockSpec(memory_space=pltpu.VMEM)
    return pl.pallas_call(
        sat_kernel,
        in_specs=[hbm, hbm, hbm, hbm, vmem],
        out_specs=[hbm, vmem, vmem, vmem, vmem],
        out_shape=[jax.ShapeDtypeStruct((2, nlon, nlat, lev), jnp.float32), lon_send, lon_send, lat_send, lat_send],
        scratch_shapes=[
            pltpu.VMEM(trajectory.shape, jnp.float32),
            pltpu.VMEM(cotangent.shape, jnp.float32),
            pltpu.VMEM(branch.shape, jnp.int32),
            pltpu.VMEM(courant.shape, jnp.float32),
            pltpu.VMEM((2, nlon, nlat, lev), jnp.float32),
            pltpu.SemaphoreType.DMA((4 * nlon // 4,)),
            pltpu.SemaphoreType.DMA((nlon // 4,)),
        ],
    )(trajectory, cotangent, branch, courant, mask)


def stencil_kernel(first_hbm, cot_hbm, cour_hbm, out_hbm, field_v, cour_v, out_v, lon_pad, lat_pad, in_sems, out_sems):
    fields, nlon, nlat, lev = cot_hbm.shape
    zeros = jnp.zeros((2, nlat, lev), jnp.float32)
    cour_copy = pltpu.make_async_copy(cour_hbm, cour_v, in_sems.at[0])
    cour_copy.start()
    loads = [pltpu.make_async_copy(first_hbm, field_v.at[0:2], in_sems.at[1])]
    loads += [pltpu.make_async_copy(cot_hbm.at[f], field_v.at[f], in_sems.at[f]) for f in range(2, fields)]
    for c in loads:
        c.start()
    lon_pad[0:2] = zeros
    lon_pad[nlon + 2:nlon + 4] = zeros
    lat_pad[6:8] = zeros[0, 0:2]
    lat_pad[8 + nlat:10 + nlat] = zeros[0, 0:2]
    cour_copy.wait()
    stores = []
    for f in range(fields):
        if f == 0:
            loads[0].wait()
        elif f >= 2:
            loads[f - 1].wait()
        src = field_v.at[f]
        for r in range(nlon):
            lon_pad[r + 2] = cour_v[0, r] * src[r]
        for r in range(nlon):
            lat_pad[8:8 + nlat] = cour_v[1, r] * src[r]
            d_lat = (8.0 * (lat_pad[9:9 + nlat] - lat_pad[7:7 + nlat]) - (lat_pad[10:10 + nlat] - lat_pad[6:6 + nlat])) / 12.0
            d_lon = (8.0 * (lon_pad[r + 3] - lon_pad[r + 1]) - (lon_pad[r + 4] - lon_pad[r])) / 12.0
            out_v[f, r] = src[r] + d_lon + d_lat
        store = pltpu.make_async_copy(out_v.at[f], out_hbm.at[f], out_sems.at[f])
        store.start()
        stores.append(store)
    for store in stores:
        store.wait()


def advect(first, cotangent, courant):
    fields, nlon, nlat, lev = cotangent.shape
    size = cotangent.size * 4
    hbm = pl.BlockSpec(memory_space=pl.ANY)
    return pl.pallas_call(
        stencil_kernel,
        in_specs=[hbm, hbm, hbm],
        out_specs=hbm,
        out_shape=jax.ShapeDtypeStruct(cotangent.shape, jnp.float32),
        scratch_shapes=[
            pltpu.VMEM(cotangent.shape, jnp.float32),
            pltpu.VMEM(courant.shape, jnp.float32),
            pltpu.VMEM(cotangent.shape, jnp.float32),
            pltpu.VMEM((nlon + 4, nlat, lev), jnp.float32),
            pltpu.VMEM((nlat + 16, lev), jnp.float32),
            pltpu.SemaphoreType.DMA((fields,)),
            pltpu.SemaphoreType.DMA((fields,)),
        ],
        cost_estimate=pl.CostEstimate(flops=12 * cotangent.size, transcendentals=0, bytes_accessed=3 * size),
    )(first, cotangent, courant)


def halo_kernel(lon_low, lon_high, lat_low, lat_high, out_hbm, out_ref,
                lon_lo_buf, lon_hi_buf, lat_lo_buf, lat_hi_buf, sems):
    fields, nlon, nlat, lev = out_hbm.shape
    regions = [
        (out_hbm.at[:, 0:2], lon_lo_buf),
        (out_hbm.at[:, nlon - 2:nlon], lon_hi_buf),
        (out_hbm.at[:, 2:nlon - 2, 0:8], lat_lo_buf),
        (out_hbm.at[:, 2:nlon - 2, nlat - 8:nlat], lat_hi_buf),
    ]
    copies = [pltpu.make_async_copy(s, d, sems.at[i]) for i, (s, d) in enumerate(regions)]
    for c in copies:
        c.start()
    for c in copies:
        c.wait()
    sub = lax.broadcasted_iota(jnp.int32, (8, lev), 0)

    def lat_fix(tile, low_rows, high_rows, at_low):
        if at_low:
            row0 = (low_rows[0:1] - 8.0 * low_rows[1:2]) / 12.0
            row1 = low_rows[1:2] / 12.0
            return tile + jnp.where(sub == 0, row0, jnp.where(sub == 1, row1, 0.0))
        row6 = -high_rows[0:1] / 12.0
        row7 = (8.0 * high_rows[0:1] - high_rows[1:2]) / 12.0
        return tile + jnp.where(sub == 6, row6, jnp.where(sub == 7, row7, 0.0))

    for f in range(fields):
        lo = lon_low[f]
        hi = lon_high[f]
        edge_terms = [(lo[0] - 8.0 * lo[1]) / 12.0, lo[1] / 12.0, -hi[0] / 12.0, (8.0 * hi[0] - hi[1]) / 12.0]
        for k, r in enumerate((0, 1, nlon - 2, nlon - 1)):
            buf = lon_lo_buf if k < 2 else lon_hi_buf
            block = buf[f, k % 2] + edge_terms[k]
            low_rows = lat_low[f, 2 * r:2 * r + 2]
            high_rows = lat_high[f, 2 * r:2 * r + 2]
            buf[f, k % 2] = block
            buf[f, k % 2, 0:8] = lat_fix(block[0:8], low_rows, high_rows, True)
            buf[f, k % 2, nlat - 8:nlat] = lat_fix(block[nlat - 8:nlat], low_rows, high_rows, False)
        for r in range(2, nlon - 2):
            low_rows = lat_low[f, 2 * r:2 * r + 2]
            high_rows = lat_high[f, 2 * r:2 * r + 2]
            lat_lo_buf[f, r - 2] = lat_fix(lat_lo_buf[f, r - 2], low_rows, high_rows, True)
            lat_hi_buf[f, r - 2] = lat_fix(lat_hi_buf[f, r - 2], low_rows, high_rows, False)
    copies = [pltpu.make_async_copy(d, s, sems.at[4 + i]) for i, (s, d) in enumerate(regions)]
    for c in copies:
        c.start()
    for c in copies:
        c.wait()


def add_halos(out, lon_low, lon_high, lat_low, lat_high):
    fields, nlon, nlat, lev = out.shape
    hbm = pl.BlockSpec(memory_space=pltpu.HBM)
    vmem = pl.BlockSpec(memory_space=pltpu.VMEM)
    return pl.pallas_call(
        halo_kernel,
        in_specs=[vmem, vmem, vmem, vmem, hbm],
        out_specs=hbm,
        out_shape=jax.ShapeDtypeStruct(out.shape, jnp.float32),
        scratch_shapes=[
            pltpu.VMEM((fields, 2, nlat, lev), jnp.float32),
            pltpu.VMEM((fields, 2, nlat, lev), jnp.float32),
            pltpu.VMEM((fields, nlon - 4, 8, lev), jnp.float32),
            pltpu.VMEM((fields, nlon - 4, 8, lev), jnp.float32),
            pltpu.SemaphoreType.DMA((8,)),
        ],
        input_output_aliases={4: 0},
    )(lon_low, lon_high, lat_low, lat_high, out)


def neighbours(axis, periodic):
    count = lax.axis_size(axis)
    forward = [(i, i + 1) for i in range(count - 1)]
    if periodic:
        forward.append((count - 1, 0))
    backward = [(target, source) for source, target in forward]
    return forward, backward


def on_device(trajectory, cotangent, courant, branch, cloud_list, cloud_count):
    fields, nlon, nlat, lev = cotangent.shape
    rows = 8
    mask = cloudy_columns(cloud_list, cloud_count, nlon, nlat, rows)
    first, lon_bottom, lon_top, lat_bottom, lat_top = first_pair(trajectory, cotangent, branch, mask, courant, rows)
    forward, backward = neighbours("lon", True)
    lon_low = lax.ppermute(lon_top, "lon", forward)
    lon_high = lax.ppermute(lon_bottom, "lon", backward)
    forward, backward = neighbours("lat", False)
    lat_low = lax.ppermute(lat_top, "lat", forward)
    lat_high = lax.ppermute(lat_bottom, "lat", backward)
    out = advect(first, cotangent, courant)
    return add_halos(out, lon_low, lon_high, lat_low, lat_high)


def solution(mesh):
    placed = (
        P(None, "lon", "lat", None),
        P(None, "lon", "lat", None),
        P(None, "lon", "lat", None),
        P("lon", "lat", None),
        P("lon", "lat", None),
        P("lon", "lat"),
    )
    return jax.shard_map(
        on_device,
        mesh=mesh,
        in_specs=placed,
        out_specs=P(None, "lon", "lat", None),
        check_vma=False,
    )
```

```python
import jax
import jax.numpy as jnp
from jax import lax
from jax.experimental import pallas as pl
from jax.experimental.pallas import tpu as pltpu
from jax.sharding import PartitionSpec as P

NEWT = 4


growth = 0.5
latent_liquid = 1.0
latent_ice = 1.3


def increments(warmth, vapour, kinds):
    mixed = jax.nn.sigmoid(2.0 * warmth)
    liquid_share = jnp.where(kinds == 1, 1.0, jnp.where(kinds == 2, 0.0, mixed))
    latent = latent_liquid * liquid_share + latent_ice * (1.0 - liquid_share)
    active = (kinds > 0).astype(warmth.dtype)
    amount = jnp.zeros_like(warmth)
    for newton_step in range(NEWT):
        saturated = jnp.exp(growth * (warmth + latent * amount))
        excess = vapour - amount - saturated
        amount = amount + excess / (1.0 + growth * latent * saturated)
    amount = active * amount
    return (latent * amount, -amount, liquid_share * amount, (1.0 - liquid_share) * amount)


def sat_adjoint(warmth, vapour, kinds, cot_heat, cot_vapour, cot_liquid, cot_ice):

    def forward(first_in, second_in):
        return increments(first_in, second_in, kinds)

    unused, pullback = jax.vjp(forward, warmth, vapour)
    grad_heat, grad_vapour = pullback((cot_heat, cot_vapour, cot_liquid, cot_ice))
    return (cot_heat + grad_heat, cot_vapour + grad_vapour)


def cloudy_columns(cloud_list, cloud_count, nlon, nlat, rows):
    index = cloud_list[0, 0]
    count = cloud_count[0, 0]
    slot = jnp.arange(index.shape[0], dtype=jnp.int32)
    hit = (index[:, None] == jnp.arange(nlon * nlat, dtype=jnp.int32)[None, :]) & (slot < count)[:, None]
    cloudy = jnp.any(hit, axis=0).astype(jnp.float32)
    return jnp.transpose(cloudy.reshape(nlon // rows, rows, nlat), (0, 2, 1))


def sat_kernel(traj_ref, cot_ref, kind_ref, mask_ref, cour_ref,
               out_ref, lon_bottom, lon_top, lat_bottom, lat_top):
    fields, rows, nlat, lev = cot_ref.shape
    step = pl.program_id(0)
    last = pl.num_programs(0) - 1
    chunk = 32
    parts = nlat // chunk
    for r in range(rows):
        after = [[None] * parts for _ in range(fields)]
        for j in range(parts):
            lat = pl.ds(j * chunk, chunk)
            cot = [cot_ref[k, r, lat, :] for k in range(4)]
            new_heat, new_vapour = sat_adjoint(
                traj_ref[0, r, lat, :], traj_ref[1, r, lat, :], kind_ref[r, lat, :], *cot
            )
            cloudy = jnp.broadcast_to(mask_ref[0, lat, r:r + 1], (chunk, lev)) > 0.0
            heat = jnp.where(cloudy, new_heat, cot[0])
            vapour = jnp.where(cloudy, new_vapour, cot[1])
            out_ref[0, r, lat, :] = heat
            out_ref[1, r, lat, :] = vapour
            after[0][j] = heat
            after[1][j] = vapour
            for f in range(2, fields):
                after[f][j] = cot_ref[f, r, lat, :]
        low_weight = cour_ref[1, r, 0:2, :]
        high_weight = cour_ref[1, r, nlat - 2:nlat, :]
        for f in range(fields):
            lat_bottom[f, 2 * r:2 * r + 2, :] = low_weight * after[f][0][0:2]
            lat_top[f, 2 * r:2 * r + 2, :] = high_weight * after[f][parts - 1][chunk - 2:chunk]
        if r < 2:
            @pl.when(step == 0)
            def _():
                for f in range(fields):
                    for j in range(parts):
                        lat = pl.ds(j * chunk, chunk)
                        lon_bottom[f, r, lat, :] = cour_ref[0, r, lat, :] * after[f][j]
        if r >= rows - 2:
            @pl.when(step == last)
            def _():
                for f in range(fields):
                    for j in range(parts):
                        lat = pl.ds(j * chunk, chunk)
                        lon_top[f, r - rows + 2, lat, :] = cour_ref[0, r, lat, :] * after[f][j]


def first_pair(trajectory, cotangent, branch, mask, courant, rows):
    fields, nlon, nlat, lev = cotangent.shape
    lon_send = jax.ShapeDtypeStruct((fields, 2, nlat, lev), jnp.float32)
    lat_send = jax.ShapeDtypeStruct((fields, 2 * nlon, lev), jnp.float32)
    return pl.pallas_call(
        sat_kernel,
        grid=(nlon // rows,),
        in_specs=[
            pl.BlockSpec((2, rows, nlat, lev), lambda i: (0, i, 0, 0)),
            pl.BlockSpec((fields, rows, nlat, lev), lambda i: (0, i, 0, 0)),
            pl.BlockSpec((rows, nlat, lev), lambda i: (i, 0, 0)),
            pl.BlockSpec((1, nlat, rows), lambda i: (i, 0, 0)),
            pl.BlockSpec((2, rows, nlat, lev), lambda i: (0, i, 0, 0)),
        ],
        out_specs=[
            pl.BlockSpec((2, rows, nlat, lev), lambda i: (0, i, 0, 0)),
            pl.BlockSpec((fields, 2, nlat, lev), lambda i: (0, 0, 0, 0)),
            pl.BlockSpec((fields, 2, nlat, lev), lambda i: (0, 0, 0, 0)),
            pl.BlockSpec((fields, 2 * rows, lev), lambda i: (0, i, 0)),
            pl.BlockSpec((fields, 2 * rows, lev), lambda i: (0, i, 0)),
        ],
        out_shape=[jax.ShapeDtypeStruct((2, nlon, nlat, lev), jnp.float32), lon_send, lon_send, lat_send, lat_send],
    )(trajectory, cotangent, branch, mask, courant)


def stencil_kernel(first_hbm, cot_hbm, cour_hbm, out_hbm, field_v, cour_v, out_v, lon_pad, lat_pad, in_sems, out_sems):
    fields, nlon, nlat, lev = cot_hbm.shape
    zeros = jnp.zeros((2, nlat, lev), jnp.float32)
    cour_copy = pltpu.make_async_copy(cour_hbm, cour_v, in_sems.at[0])
    cour_copy.start()
    loads = [pltpu.make_async_copy(first_hbm, field_v.at[0:2], in_sems.at[1])]
    loads += [pltpu.make_async_copy(cot_hbm.at[f], field_v.at[f], in_sems.at[f]) for f in range(2, fields)]
    for c in loads:
        c.start()
    lon_pad[0:2] = zeros
    lon_pad[nlon + 2:nlon + 4] = zeros
    lat_pad[6:8] = zeros[0, 0:2]
    lat_pad[8 + nlat:10 + nlat] = zeros[0, 0:2]
    cour_copy.wait()
    stores = []
    for f in range(fields):
        if f == 0:
            loads[0].wait()
        elif f >= 2:
            loads[f - 1].wait()
        src = field_v.at[f]
        for r in range(nlon):
            lon_pad[r + 2] = cour_v[0, r] * src[r]
        for r in range(nlon):
            lat_pad[8:8 + nlat] = cour_v[1, r] * src[r]
            d_lat = (8.0 * (lat_pad[9:9 + nlat] - lat_pad[7:7 + nlat]) - (lat_pad[10:10 + nlat] - lat_pad[6:6 + nlat])) / 12.0
            d_lon = (8.0 * (lon_pad[r + 3] - lon_pad[r + 1]) - (lon_pad[r + 4] - lon_pad[r])) / 12.0
            out_v[f, r] = src[r] + d_lon + d_lat
        store = pltpu.make_async_copy(out_v.at[f], out_hbm.at[f], out_sems.at[f])
        store.start()
        stores.append(store)
    for store in stores:
        store.wait()


def advect(first, cotangent, courant):
    fields, nlon, nlat, lev = cotangent.shape
    size = cotangent.size * 4
    hbm = pl.BlockSpec(memory_space=pl.ANY)
    return pl.pallas_call(
        stencil_kernel,
        in_specs=[hbm, hbm, hbm],
        out_specs=hbm,
        out_shape=jax.ShapeDtypeStruct(cotangent.shape, jnp.float32),
        scratch_shapes=[
            pltpu.VMEM(cotangent.shape, jnp.float32),
            pltpu.VMEM(courant.shape, jnp.float32),
            pltpu.VMEM(cotangent.shape, jnp.float32),
            pltpu.VMEM((nlon + 4, nlat, lev), jnp.float32),
            pltpu.VMEM((nlat + 16, lev), jnp.float32),
            pltpu.SemaphoreType.DMA((fields,)),
            pltpu.SemaphoreType.DMA((fields,)),
        ],
        cost_estimate=pl.CostEstimate(flops=12 * cotangent.size, transcendentals=0, bytes_accessed=3 * size),
    )(first, cotangent, courant)


def halo_kernel(lon_low_hbm, lon_high_hbm, lat_low_hbm, lat_high_hbm, out_hbm, out_ref,
                lon_low, lon_high, lat_low, lat_high, lon_lo_buf, lon_hi_buf, lat_lo_buf, lat_hi_buf, sems, in_sems, out_sems):
    fields, nlon, nlat, lev = out_hbm.shape
    halos = [(lon_low_hbm, lon_low), (lon_high_hbm, lon_high), (lat_low_hbm, lat_low), (lat_high_hbm, lat_high)]
    halo_copies = [pltpu.make_async_copy(s, d, sems.at[i]) for i, (s, d) in enumerate(halos)]
    for c in halo_copies:
        c.start()

    def regions(f):
        return [
            (out_hbm.at[f, 0:2], lon_lo_buf.at[f]),
            (out_hbm.at[f, nlon - 2:nlon], lon_hi_buf.at[f]),
            (out_hbm.at[f, 2:nlon - 2, 0:8], lat_lo_buf.at[f]),
            (out_hbm.at[f, 2:nlon - 2, nlat - 8:nlat], lat_hi_buf.at[f]),
        ]

    loads = []
    for f in range(fields):
        copies = [pltpu.make_async_copy(s, d, in_sems.at[4 * f + i]) for i, (s, d) in enumerate(regions(f))]
        for c in copies:
            c.start()
        loads.append(copies)
    for c in halo_copies:
        c.wait()
    sub = lax.broadcasted_iota(jnp.int32, (8, lev), 0)

    def lat_fix(tile, low_rows, high_rows, at_low):
        if at_low:
            row0 = (low_rows[0:1] - 8.0 * low_rows[1:2]) / 12.0
            row1 = low_rows[1:2] / 12.0
            return tile + jnp.where(sub == 0, row0, jnp.where(sub == 1, row1, 0.0))
        row6 = -high_rows[0:1] / 12.0
        row7 = (8.0 * high_rows[0:1] - high_rows[1:2]) / 12.0
        return tile + jnp.where(sub == 6, row6, jnp.where(sub == 7, row7, 0.0))

    stores = []
    for f in range(fields):
        for c in loads[f]:
            c.wait()
        lo = lon_low[f]
        hi = lon_high[f]
        edge_terms = [(lo[0] - 8.0 * lo[1]) / 12.0, lo[1] / 12.0, -hi[0] / 12.0, (8.0 * hi[0] - hi[1]) / 12.0]
        for k, r in enumerate((0, 1, nlon - 2, nlon - 1)):
            buf = lon_lo_buf if k < 2 else lon_hi_buf
            block = buf[f, k % 2] + edge_terms[k]
            low_rows = lat_low[f, 2 * r:2 * r + 2]
            high_rows = lat_high[f, 2 * r:2 * r + 2]
            buf[f, k % 2] = block
            buf[f, k % 2, 0:8] = lat_fix(block[0:8], low_rows, high_rows, True)
            buf[f, k % 2, nlat - 8:nlat] = lat_fix(block[nlat - 8:nlat], low_rows, high_rows, False)
        for r in range(2, nlon - 2):
            low_rows = lat_low[f, 2 * r:2 * r + 2]
            high_rows = lat_high[f, 2 * r:2 * r + 2]
            lat_lo_buf[f, r - 2] = lat_fix(lat_lo_buf[f, r - 2], low_rows, high_rows, True)
            lat_hi_buf[f, r - 2] = lat_fix(lat_hi_buf[f, r - 2], low_rows, high_rows, False)
        copies = [pltpu.make_async_copy(d, s, out_sems.at[4 * f + i]) for i, (s, d) in enumerate(regions(f))]
        for c in copies:
            c.start()
        stores += copies
    for c in stores:
        c.wait()


def add_halos(out, lon_low, lon_high, lat_low, lat_high):
    fields, nlon, nlat, lev = out.shape
    hbm = pl.BlockSpec(memory_space=pl.ANY)
    return pl.pallas_call(
        halo_kernel,
        in_specs=[hbm] * 5,
        out_specs=hbm,
        out_shape=jax.ShapeDtypeStruct(out.shape, jnp.float32),
        scratch_shapes=[
            pltpu.VMEM(lon_low.shape, jnp.float32),
            pltpu.VMEM(lon_high.shape, jnp.float32),
            pltpu.VMEM(lat_low.shape, jnp.float32),
            pltpu.VMEM(lat_high.shape, jnp.float32),
            pltpu.VMEM((fields, 2, nlat, lev), jnp.float32),
            pltpu.VMEM((fields, 2, nlat, lev), jnp.float32),
            pltpu.VMEM((fields, nlon - 4, 8, lev), jnp.float32),
            pltpu.VMEM((fields, nlon - 4, 8, lev), jnp.float32),
            pltpu.SemaphoreType.DMA((4,)),
            pltpu.SemaphoreType.DMA((4 * fields,)),
            pltpu.SemaphoreType.DMA((4 * fields,)),
        ],
        input_output_aliases={4: 0},
    )(lon_low, lon_high, lat_low, lat_high, out)


def neighbours(axis, periodic):
    count = lax.axis_size(axis)
    forward = [(i, i + 1) for i in range(count - 1)]
    if periodic:
        forward.append((count - 1, 0))
    backward = [(target, source) for source, target in forward]
    return forward, backward


def on_device(trajectory, cotangent, courant, branch, cloud_list, cloud_count):
    fields, nlon, nlat, lev = cotangent.shape
    rows = 8
    mask = cloudy_columns(cloud_list, cloud_count, nlon, nlat, rows)
    first, lon_bottom, lon_top, lat_bottom, lat_top = first_pair(trajectory, cotangent, branch, mask, courant, rows)
    forward, backward = neighbours("lat", False)
    lat_low = lax.ppermute(lat_top, "lat", forward)
    lat_high = lax.ppermute(lat_bottom, "lat", backward)
    forward, backward = neighbours("lon", True)
    lon_high = lax.ppermute(lon_bottom, "lon", backward)
    lon_low = lax.ppermute(lon_top, "lon", forward)
    out = advect(first, cotangent, courant)
    return add_halos(out, lon_low, lon_high, lat_low, lat_high)


def solution(mesh):
    placed = (
        P(None, "lon", "lat", None),
        P(None, "lon", "lat", None),
        P(None, "lon", "lat", None),
        P("lon", "lat", None),
        P("lon", "lat", None),
        P("lon", "lat"),
    )
    return jax.shard_map(
        on_device,
        mesh=mesh,
        in_specs=placed,
        out_specs=P(None, "lon", "lat", None),
        check_vma=False,
    )
```

```python
import jax
import jax.numpy as jnp
from jax import lax
from jax.experimental import pallas as pl
from jax.experimental.pallas import tpu as pltpu
from jax.sharding import PartitionSpec as P

NEWT = 4


growth = 0.5
latent_liquid = 1.0
latent_ice = 1.3


def sat_adjoint(warmth, vapour, kinds, cot_heat, cot_vapour, cot_liquid, cot_ice):
    mixed = jax.nn.sigmoid(2.0 * warmth)
    liquid_share = jnp.where(kinds == 1, 1.0, jnp.where(kinds == 2, 0.0, mixed))
    latent = latent_liquid * liquid_share + latent_ice * (1.0 - liquid_share)
    active = (kinds > 0).astype(warmth.dtype)
    half_latent = growth * latent
    amount = jnp.zeros_like(warmth)
    saved = []
    for newton_step in range(NEWT):
        saturated = jnp.exp(growth * (warmth + latent * amount))
        inverse = 1.0 / (1.0 + half_latent * saturated)
        excess = vapour - amount - saturated
        saved.append((amount, saturated, inverse, excess))
        amount = amount + excess * inverse
    amount = active * amount
    grad_amount = latent * cot_heat - cot_vapour + liquid_share * cot_liquid + (1.0 - liquid_share) * cot_ice
    grad_share = amount * (cot_liquid - cot_ice)
    grad_latent = amount * cot_heat
    grad = active * grad_amount
    grad_heat = jnp.zeros_like(warmth)
    grad_vapour = jnp.zeros_like(warmth)
    for amount, saturated, inverse, excess in reversed(saved):
        slope = excess * inverse * inverse
        grad_sat = -grad * (inverse + half_latent * slope)
        half_sat = growth * saturated
        grad_heat = grad_heat + grad_sat * half_sat
        grad_latent = grad_latent + grad_sat * half_sat * amount - grad * slope * half_sat
        grad_vapour = grad_vapour + grad * inverse
        grad = grad * (1.0 - inverse) + grad_sat * half_latent * saturated
    grad_share = grad_share + (latent_liquid - latent_ice) * grad_latent
    mixed_kind = (kinds == 0) | (kinds == 3)
    grad_heat = grad_heat + jnp.where(mixed_kind, grad_share * 2.0 * mixed * (1.0 - mixed), 0.0)
    return (cot_heat + grad_heat, cot_vapour + grad_vapour)


def cloudy_columns(cloud_list, cloud_count, nlon, nlat, rows):
    index = cloud_list[0, 0]
    count = cloud_count[0, 0]
    slot = jnp.arange(index.shape[0], dtype=jnp.int32)
    hit = (index[:, None] == jnp.arange(nlon * nlat, dtype=jnp.int32)[None, :]) & (slot < count)[:, None]
    cloudy = jnp.any(hit, axis=0).astype(jnp.float32)
    return jnp.transpose(cloudy.reshape(nlon // rows, rows, nlat), (0, 2, 1))


def sat_kernel(traj_ref, cot_ref, kind_ref, mask_ref, cour_ref,
               out_ref, lon_bottom, lon_top, lat_bottom, lat_top):
    fields, rows, nlat, lev = cot_ref.shape
    step = pl.program_id(0)
    last = pl.num_programs(0) - 1
    chunk = 32
    parts = nlat // chunk
    for r in range(rows):
        after = [[None] * parts for _ in range(fields)]
        for j in range(parts):
            lat = pl.ds(j * chunk, chunk)
            cot = [cot_ref[k, r, lat, :] for k in range(4)]
            new_heat, new_vapour = sat_adjoint(
                traj_ref[0, r, lat, :], traj_ref[1, r, lat, :], kind_ref[r, lat, :], *cot
            )
            cloudy = jnp.broadcast_to(mask_ref[0, lat, r:r + 1], (chunk, lev)) > 0.0
            heat = jnp.where(cloudy, new_heat, cot[0])
            vapour = jnp.where(cloudy, new_vapour, cot[1])
            out_ref[0, r, lat, :] = heat
            out_ref[1, r, lat, :] = vapour
            after[0][j] = heat
            after[1][j] = vapour
            for f in range(2, fields):
                after[f][j] = cot_ref[f, r, lat, :]
        low_weight = cour_ref[1, r, 0:2, :]
        high_weight = cour_ref[1, r, nlat - 2:nlat, :]
        for f in range(fields):
            lat_bottom[f, 2 * r:2 * r + 2, :] = low_weight * after[f][0][0:2]
            lat_top[f, 2 * r:2 * r + 2, :] = high_weight * after[f][parts - 1][chunk - 2:chunk]
        if r < 2:
            @pl.when(step == 0)
            def _():
                for f in range(fields):
                    for j in range(parts):
                        lat = pl.ds(j * chunk, chunk)
                        lon_bottom[f, r, lat, :] = cour_ref[0, r, lat, :] * after[f][j]
        if r >= rows - 2:
            @pl.when(step == last)
            def _():
                for f in range(fields):
                    for j in range(parts):
                        lat = pl.ds(j * chunk, chunk)
                        lon_top[f, r - rows + 2, lat, :] = cour_ref[0, r, lat, :] * after[f][j]


def first_pair(trajectory, cotangent, branch, mask, courant, rows):
    fields, nlon, nlat, lev = cotangent.shape
    lon_send = jax.ShapeDtypeStruct((fields, 2, nlat, lev), jnp.float32)
    lat_send = jax.ShapeDtypeStruct((fields, 2 * nlon, lev), jnp.float32)
    return pl.pallas_call(
        sat_kernel,
        grid=(nlon // rows,),
        in_specs=[
            pl.BlockSpec((2, rows, nlat, lev), lambda i: (0, i, 0, 0)),
            pl.BlockSpec((fields, rows, nlat, lev), lambda i: (0, i, 0, 0)),
            pl.BlockSpec((rows, nlat, lev), lambda i: (i, 0, 0)),
            pl.BlockSpec((1, nlat, rows), lambda i: (i, 0, 0)),
            pl.BlockSpec((2, rows, nlat, lev), lambda i: (0, i, 0, 0)),
        ],
        out_specs=[
            pl.BlockSpec((2, rows, nlat, lev), lambda i: (0, i, 0, 0)),
            pl.BlockSpec((fields, 2, nlat, lev), lambda i: (0, 0, 0, 0)),
            pl.BlockSpec((fields, 2, nlat, lev), lambda i: (0, 0, 0, 0)),
            pl.BlockSpec((fields, 2 * rows, lev), lambda i: (0, i, 0)),
            pl.BlockSpec((fields, 2 * rows, lev), lambda i: (0, i, 0)),
        ],
        out_shape=[jax.ShapeDtypeStruct((2, nlon, nlat, lev), jnp.float32), lon_send, lon_send, lat_send, lat_send],
    )(trajectory, cotangent, branch, mask, courant)


def stencil_kernel(first_hbm, cot_hbm, cour_hbm, out_hbm, field_v, cour_v, out_v, lon_pad, lat_pad, in_sems, out_sems):
    fields, nlon, nlat, lev = cot_hbm.shape
    zeros = jnp.zeros((2, nlat, lev), jnp.float32)
    cour_copy = pltpu.make_async_copy(cour_hbm, cour_v, in_sems.at[0])
    cour_copy.start()
    loads = [pltpu.make_async_copy(first_hbm, field_v.at[0:2], in_sems.at[1])]
    loads += [pltpu.make_async_copy(cot_hbm.at[f], field_v.at[f], in_sems.at[f]) for f in range(2, fields)]
    for c in loads:
        c.start()
    lon_pad[0:2] = zeros
    lon_pad[nlon + 2:nlon + 4] = zeros
    lat_pad[6:8] = zeros[0, 0:2]
    lat_pad[8 + nlat:10 + nlat] = zeros[0, 0:2]
    cour_copy.wait()
    stores = []
    for f in range(fields):
        if f == 0:
            loads[0].wait()
        elif f >= 2:
            loads[f - 1].wait()
        src = field_v.at[f]
        for r in range(nlon):
            lon_pad[r + 2] = cour_v[0, r] * src[r]
        for r in range(nlon):
            lat_pad[8:8 + nlat] = cour_v[1, r] * src[r]
            d_lat = (8.0 * (lat_pad[9:9 + nlat] - lat_pad[7:7 + nlat]) - (lat_pad[10:10 + nlat] - lat_pad[6:6 + nlat])) / 12.0
            d_lon = (8.0 * (lon_pad[r + 3] - lon_pad[r + 1]) - (lon_pad[r + 4] - lon_pad[r])) / 12.0
            out_v[f, r] = src[r] + d_lon + d_lat
        store = pltpu.make_async_copy(out_v.at[f], out_hbm.at[f], out_sems.at[f])
        store.start()
        stores.append(store)
    for store in stores:
        store.wait()


def advect(first, cotangent, courant):
    fields, nlon, nlat, lev = cotangent.shape
    size = cotangent.size * 4
    hbm = pl.BlockSpec(memory_space=pl.ANY)
    return pl.pallas_call(
        stencil_kernel,
        in_specs=[hbm, hbm, hbm],
        out_specs=hbm,
        out_shape=jax.ShapeDtypeStruct(cotangent.shape, jnp.float32),
        scratch_shapes=[
            pltpu.VMEM(cotangent.shape, jnp.float32),
            pltpu.VMEM(courant.shape, jnp.float32),
            pltpu.VMEM(cotangent.shape, jnp.float32),
            pltpu.VMEM((nlon + 4, nlat, lev), jnp.float32),
            pltpu.VMEM((nlat + 16, lev), jnp.float32),
            pltpu.SemaphoreType.DMA((fields,)),
            pltpu.SemaphoreType.DMA((fields,)),
        ],
        cost_estimate=pl.CostEstimate(flops=12 * cotangent.size, transcendentals=0, bytes_accessed=3 * size),
    )(first, cotangent, courant)


def halo_kernel(lon_low_hbm, lon_high_hbm, lat_low_hbm, lat_high_hbm, out_hbm, out_ref,
                lon_low, lon_high, lat_low, lat_high, lon_lo_buf, lon_hi_buf, lat_lo_buf, lat_hi_buf, sems):
    fields, nlon, nlat, lev = out_hbm.shape
    halos = [(lon_low_hbm, lon_low), (lon_high_hbm, lon_high), (lat_low_hbm, lat_low), (lat_high_hbm, lat_high)]
    regions = [
        (out_hbm.at[:, 0:2], lon_lo_buf),
        (out_hbm.at[:, nlon - 2:nlon], lon_hi_buf),
        (out_hbm.at[:, 2:nlon - 2, 0:8], lat_lo_buf),
        (out_hbm.at[:, 2:nlon - 2, nlat - 8:nlat], lat_hi_buf),
    ]
    copies = [pltpu.make_async_copy(s, d, sems.at[i]) for i, (s, d) in enumerate(halos + regions)]
    for c in copies:
        c.start()
    for c in copies:
        c.wait()
    sub = lax.broadcasted_iota(jnp.int32, (8, lev), 0)

    def lat_fix(tile, low_rows, high_rows, at_low):
        if at_low:
            row0 = (low_rows[0:1] - 8.0 * low_rows[1:2]) / 12.0
            row1 = low_rows[1:2] / 12.0
            return tile + jnp.where(sub == 0, row0, jnp.where(sub == 1, row1, 0.0))
        row6 = -high_rows[0:1] / 12.0
        row7 = (8.0 * high_rows[0:1] - high_rows[1:2]) / 12.0
        return tile + jnp.where(sub == 6, row6, jnp.where(sub == 7, row7, 0.0))

    for f in range(fields):
        lo = lon_low[f]
        hi = lon_high[f]
        edge_terms = [(lo[0] - 8.0 * lo[1]) / 12.0, lo[1] / 12.0, -hi[0] / 12.0, (8.0 * hi[0] - hi[1]) / 12.0]
        for k, r in enumerate((0, 1, nlon - 2, nlon - 1)):
            buf = lon_lo_buf if k < 2 else lon_hi_buf
            block = buf[f, k % 2] + edge_terms[k]
            low_rows = lat_low[f, 2 * r:2 * r + 2]
            high_rows = lat_high[f, 2 * r:2 * r + 2]
            buf[f, k % 2] = block
            buf[f, k % 2, 0:8] = lat_fix(block[0:8], low_rows, high_rows, True)
            buf[f, k % 2, nlat - 8:nlat] = lat_fix(block[nlat - 8:nlat], low_rows, high_rows, False)
        for r in range(2, nlon - 2):
            low_rows = lat_low[f, 2 * r:2 * r + 2]
            high_rows = lat_high[f, 2 * r:2 * r + 2]
            lat_lo_buf[f, r - 2] = lat_fix(lat_lo_buf[f, r - 2], low_rows, high_rows, True)
            lat_hi_buf[f, r - 2] = lat_fix(lat_hi_buf[f, r - 2], low_rows, high_rows, False)
    copies = [pltpu.make_async_copy(d, s, sems.at[4 + i]) for i, (s, d) in enumerate(regions)]
    for c in copies:
        c.start()
    for c in copies:
        c.wait()


def add_halos(out, lon_low, lon_high, lat_low, lat_high):
    fields, nlon, nlat, lev = out.shape
    hbm = pl.BlockSpec(memory_space=pl.ANY)
    return pl.pallas_call(
        halo_kernel,
        in_specs=[hbm] * 5,
        out_specs=hbm,
        out_shape=jax.ShapeDtypeStruct(out.shape, jnp.float32),
        scratch_shapes=[
            pltpu.VMEM(lon_low.shape, jnp.float32),
            pltpu.VMEM(lon_high.shape, jnp.float32),
            pltpu.VMEM(lat_low.shape, jnp.float32),
            pltpu.VMEM(lat_high.shape, jnp.float32),
            pltpu.VMEM((fields, 2, nlat, lev), jnp.float32),
            pltpu.VMEM((fields, 2, nlat, lev), jnp.float32),
            pltpu.VMEM((fields, nlon - 4, 8, lev), jnp.float32),
            pltpu.VMEM((fields, nlon - 4, 8, lev), jnp.float32),
            pltpu.SemaphoreType.DMA((8,)),
        ],
        input_output_aliases={4: 0},
    )(lon_low, lon_high, lat_low, lat_high, out)


def neighbours(axis, periodic):
    count = lax.axis_size(axis)
    forward = [(i, i + 1) for i in range(count - 1)]
    if periodic:
        forward.append((count - 1, 0))
    backward = [(target, source) for source, target in forward]
    return forward, backward


def on_device(trajectory, cotangent, courant, branch, cloud_list, cloud_count):
    fields, nlon, nlat, lev = cotangent.shape
    rows = 8
    mask = cloudy_columns(cloud_list, cloud_count, nlon, nlat, rows)
    first, lon_bottom, lon_top, lat_bottom, lat_top = first_pair(trajectory, cotangent, branch, mask, courant, rows)
    forward, backward = neighbours("lon", True)
    lon_low = lax.ppermute(lon_top, "lon", forward)
    lon_high = lax.ppermute(lon_bottom, "lon", backward)
    forward, backward = neighbours("lat", False)
    lat_low = lax.ppermute(lat_top, "lat", forward)
    lat_high = lax.ppermute(lat_bottom, "lat", backward)
    out = advect(first, cotangent, courant)
    return add_halos(out, lon_low, lon_high, lat_low, lat_high)


def solution(mesh):
    placed = (
        P(None, "lon", "lat", None),
        P(None, "lon", "lat", None),
        P(None, "lon", "lat", None),
        P("lon", "lat", None),
        P("lon", "lat", None),
        P("lon", "lat"),
    )
    return jax.shard_map(
        on_device,
        mesh=mesh,
        in_specs=placed,
        out_specs=P(None, "lon", "lat", None),
        check_vma=False,
    )
```

```python
import jax
import jax.numpy as jnp
from jax import lax
from jax.experimental import pallas as pl
from jax.experimental.pallas import tpu as pltpu
from jax.sharding import PartitionSpec as P

NEWT = 4


growth = 0.5
latent_liquid = 1.0
latent_ice = 1.3


def sat_adjoint(warmth, vapour, kinds, cot_heat, cot_vapour, cot_liquid, cot_ice):
    mixed = jax.nn.sigmoid(2.0 * warmth)
    liquid_share = jnp.where(kinds == 1, 1.0, jnp.where(kinds == 2, 0.0, mixed))
    latent = latent_liquid * liquid_share + latent_ice * (1.0 - liquid_share)
    active = (kinds > 0).astype(warmth.dtype)
    half_latent = growth * latent
    amount = jnp.zeros_like(warmth)
    saved = []
    for newton_step in range(NEWT):
        saturated = jnp.exp(growth * (warmth + latent * amount))
        inverse = 1.0 / (1.0 + half_latent * saturated)
        excess = vapour - amount - saturated
        saved.append((amount, saturated, inverse, excess))
        amount = amount + excess * inverse
    amount = active * amount
    grad_amount = latent * cot_heat - cot_vapour + liquid_share * cot_liquid + (1.0 - liquid_share) * cot_ice
    grad_share = amount * (cot_liquid - cot_ice)
    grad_latent = amount * cot_heat
    grad = active * grad_amount
    grad_heat = jnp.zeros_like(warmth)
    grad_vapour = jnp.zeros_like(warmth)
    for amount, saturated, inverse, excess in reversed(saved):
        slope = excess * inverse * inverse
        grad_sat = -grad * (inverse + half_latent * slope)
        half_sat = growth * saturated
        grad_heat = grad_heat + grad_sat * half_sat
        grad_latent = grad_latent + grad_sat * half_sat * amount - grad * slope * half_sat
        grad_vapour = grad_vapour + grad * inverse
        grad = grad * (1.0 - inverse) + grad_sat * half_latent * saturated
    grad_share = grad_share + (latent_liquid - latent_ice) * grad_latent
    mixed_kind = (kinds == 0) | (kinds == 3)
    grad_heat = grad_heat + jnp.where(mixed_kind, grad_share * 2.0 * mixed * (1.0 - mixed), 0.0)
    return (cot_heat + grad_heat, cot_vapour + grad_vapour)


def cloudy_columns(cloud_list, cloud_count, nlon, nlat, rows):
    index = cloud_list[0, 0]
    count = cloud_count[0, 0]
    slot = jnp.arange(index.shape[0], dtype=jnp.int32)
    hit = (index[:, None] == jnp.arange(nlon * nlat, dtype=jnp.int32)[None, :]) & (slot < count)[:, None]
    cloudy = jnp.any(hit, axis=0).astype(jnp.float32)
    return jnp.transpose(cloudy.reshape(nlon // rows, rows, nlat), (0, 2, 1))


def sat_kernel(parity_ref, traj_ref, cot_ref, kind_ref, mask_ref, cour_ref,
               out_ref, lon_mate, lon_far, lat_mate, lat_far):
    fields, rows, nlat, lev = cot_ref.shape
    step = pl.program_id(0)
    last = pl.num_programs(0) - 1
    chunk = 32
    parts = nlat // chunk
    for r in range(rows):
        after = [[None] * parts for _ in range(fields)]
        for j in range(parts):
            lat = pl.ds(j * chunk, chunk)
            cot = [cot_ref[k, r, lat, :] for k in range(4)]
            new_heat, new_vapour = sat_adjoint(
                traj_ref[0, r, lat, :], traj_ref[1, r, lat, :], kind_ref[r, lat, :], *cot
            )
            cloudy = jnp.broadcast_to(mask_ref[0, lat, r:r + 1], (chunk, lev)) > 0.0
            heat = jnp.where(cloudy, new_heat, cot[0])
            vapour = jnp.where(cloudy, new_vapour, cot[1])
            out_ref[0, r, lat, :] = heat
            out_ref[1, r, lat, :] = vapour
            after[0][j] = heat
            after[1][j] = vapour
            for f in range(2, fields):
                after[f][j] = cot_ref[f, r, lat, :]
        low_weight = cour_ref[1, r, 0:2, :]
        high_weight = cour_ref[1, r, nlat - 2:nlat, :]
        lat_even = parity_ref[1] == 0
        for f in range(fields):
            bottom = low_weight * after[f][0][0:2]
            top = high_weight * after[f][parts - 1][chunk - 2:chunk]
            lat_mate[f, 2 * r:2 * r + 2, :] = jnp.where(lat_even, top, bottom)
            lat_far[f, 2 * r:2 * r + 2, :] = jnp.where(lat_even, bottom, top)
        lon_even = parity_ref[0] == 0
        for edge_step, edge_rows, mate_when in ((0, range(2), jnp.logical_not(lon_even)), (last, range(rows - 2, rows), lon_even)):
            if r not in edge_rows:
                continue
            at = r - edge_rows[0]
            for target, flag in ((lon_mate, mate_when), (lon_far, jnp.logical_not(mate_when))):
                @pl.when((step == edge_step) & flag)
                def _():
                    for f in range(fields):
                        for j in range(parts):
                            lat = pl.ds(j * chunk, chunk)
                            target[f, at, lat, :] = cour_ref[0, r, lat, :] * after[f][j]


def first_pair(parity, trajectory, cotangent, branch, mask, courant, rows):
    fields, nlon, nlat, lev = cotangent.shape
    lon_send = jax.ShapeDtypeStruct((fields, 2, nlat, lev), jnp.float32)
    lat_send = jax.ShapeDtypeStruct((fields, 2 * nlon, lev), jnp.float32)
    return pl.pallas_call(
        sat_kernel,
        grid=(nlon // rows,),
        in_specs=[
            pl.BlockSpec(memory_space=pltpu.SMEM),
            pl.BlockSpec((2, rows, nlat, lev), lambda i: (0, i, 0, 0)),
            pl.BlockSpec((fields, rows, nlat, lev), lambda i: (0, i, 0, 0)),
            pl.BlockSpec((rows, nlat, lev), lambda i: (i, 0, 0)),
            pl.BlockSpec((1, nlat, rows), lambda i: (i, 0, 0)),
            pl.BlockSpec((2, rows, nlat, lev), lambda i: (0, i, 0, 0)),
        ],
        out_specs=[
            pl.BlockSpec((2, rows, nlat, lev), lambda i: (0, i, 0, 0)),
            pl.BlockSpec((fields, 2, nlat, lev), lambda i: (0, 0, 0, 0)),
            pl.BlockSpec((fields, 2, nlat, lev), lambda i: (0, 0, 0, 0)),
            pl.BlockSpec((fields, 2 * rows, lev), lambda i: (0, i, 0)),
            pl.BlockSpec((fields, 2 * rows, lev), lambda i: (0, i, 0)),
        ],
        out_shape=[jax.ShapeDtypeStruct((2, nlon, nlat, lev), jnp.float32), lon_send, lon_send, lat_send, lat_send],
    )(parity, trajectory, cotangent, branch, mask, courant)


def stencil_kernel(first_hbm, cot_hbm, cour_hbm, out_hbm, field_v, cour_v, out_v, lon_pad, lat_pad, in_sems, out_sems):
    fields, nlon, nlat, lev = cot_hbm.shape
    zeros = jnp.zeros((2, nlat, lev), jnp.float32)
    cour_copy = pltpu.make_async_copy(cour_hbm, cour_v, in_sems.at[0])
    cour_copy.start()
    loads = [pltpu.make_async_copy(first_hbm, field_v.at[0:2], in_sems.at[1])]
    loads += [pltpu.make_async_copy(cot_hbm.at[f], field_v.at[f], in_sems.at[f]) for f in range(2, fields)]
    for c in loads:
        c.start()
    lon_pad[0:2] = zeros
    lon_pad[nlon + 2:nlon + 4] = zeros
    lat_pad[6:8] = zeros[0, 0:2]
    lat_pad[8 + nlat:10 + nlat] = zeros[0, 0:2]
    cour_copy.wait()
    stores = []
    for f in range(fields):
        if f == 0:
            loads[0].wait()
        elif f >= 2:
            loads[f - 1].wait()
        src = field_v.at[f]
        for r in range(nlon):
            lon_pad[r + 2] = cour_v[0, r] * src[r]
        for r in range(nlon):
            lat_pad[8:8 + nlat] = cour_v[1, r] * src[r]
            d_lat = (8.0 * (lat_pad[9:9 + nlat] - lat_pad[7:7 + nlat]) - (lat_pad[10:10 + nlat] - lat_pad[6:6 + nlat])) / 12.0
            d_lon = (8.0 * (lon_pad[r + 3] - lon_pad[r + 1]) - (lon_pad[r + 4] - lon_pad[r])) / 12.0
            out_v[f, r] = src[r] + d_lon + d_lat
        store = pltpu.make_async_copy(out_v.at[f], out_hbm.at[f], out_sems.at[f])
        store.start()
        stores.append(store)
    for store in stores:
        store.wait()


def advect(first, cotangent, courant):
    fields, nlon, nlat, lev = cotangent.shape
    size = cotangent.size * 4
    hbm = pl.BlockSpec(memory_space=pl.ANY)
    return pl.pallas_call(
        stencil_kernel,
        in_specs=[hbm, hbm, hbm],
        out_specs=hbm,
        out_shape=jax.ShapeDtypeStruct(cotangent.shape, jnp.float32),
        scratch_shapes=[
            pltpu.VMEM(cotangent.shape, jnp.float32),
            pltpu.VMEM(courant.shape, jnp.float32),
            pltpu.VMEM(cotangent.shape, jnp.float32),
            pltpu.VMEM((nlon + 4, nlat, lev), jnp.float32),
            pltpu.VMEM((nlat + 16, lev), jnp.float32),
            pltpu.SemaphoreType.DMA((fields,)),
            pltpu.SemaphoreType.DMA((fields,)),
        ],
        cost_estimate=pl.CostEstimate(flops=12 * cotangent.size, transcendentals=0, bytes_accessed=3 * size),
    )(first, cotangent, courant)


def halo_kernel(parity_ref, lon_mate_hbm, lon_far_hbm, lat_mate_hbm, lat_far_hbm, out_hbm, out_ref,
                lon_mate, lon_far, lat_mate, lat_far, lon_lo_buf, lon_hi_buf, lat_lo_buf, lat_hi_buf, sems):
    fields, nlon, nlat, lev = out_hbm.shape
    halos = [(lon_mate_hbm, lon_mate), (lon_far_hbm, lon_far), (lat_mate_hbm, lat_mate), (lat_far_hbm, lat_far)]
    lon_even = parity_ref[0] == 0
    lat_even = parity_ref[1] == 0
    regions = [
        (out_hbm.at[:, 0:2], lon_lo_buf),
        (out_hbm.at[:, nlon - 2:nlon], lon_hi_buf),
        (out_hbm.at[:, 2:nlon - 2, 0:8], lat_lo_buf),
        (out_hbm.at[:, 2:nlon - 2, nlat - 8:nlat], lat_hi_buf),
    ]
    copies = [pltpu.make_async_copy(s, d, sems.at[i]) for i, (s, d) in enumerate(halos + regions)]
    for c in copies:
        c.start()
    for c in copies:
        c.wait()
    sub = lax.broadcasted_iota(jnp.int32, (8, lev), 0)

    def lat_fix(tile, low_rows, high_rows, at_low):
        if at_low:
            row0 = (low_rows[0:1] - 8.0 * low_rows[1:2]) / 12.0
            row1 = low_rows[1:2] / 12.0
            return tile + jnp.where(sub == 0, row0, jnp.where(sub == 1, row1, 0.0))
        row6 = -high_rows[0:1] / 12.0
        row7 = (8.0 * high_rows[0:1] - high_rows[1:2]) / 12.0
        return tile + jnp.where(sub == 6, row6, jnp.where(sub == 7, row7, 0.0))

    for f in range(fields):
        lo = jnp.where(lon_even, lon_far[f], lon_mate[f])
        hi = jnp.where(lon_even, lon_mate[f], lon_far[f])
        edge_terms = [(lo[0] - 8.0 * lo[1]) / 12.0, lo[1] / 12.0, -hi[0] / 12.0, (8.0 * hi[0] - hi[1]) / 12.0]
        for k, r in enumerate((0, 1, nlon - 2, nlon - 1)):
            buf = lon_lo_buf if k < 2 else lon_hi_buf
            block = buf[f, k % 2] + edge_terms[k]
            low_rows = jnp.where(lat_even, lat_far[f, 2 * r:2 * r + 2], lat_mate[f, 2 * r:2 * r + 2])
            high_rows = jnp.where(lat_even, lat_mate[f, 2 * r:2 * r + 2], lat_far[f, 2 * r:2 * r + 2])
            buf[f, k % 2] = block
            buf[f, k % 2, 0:8] = lat_fix(block[0:8], low_rows, high_rows, True)
            buf[f, k % 2, nlat - 8:nlat] = lat_fix(block[nlat - 8:nlat], low_rows, high_rows, False)
        for r in range(2, nlon - 2):
            low_rows = jnp.where(lat_even, lat_far[f, 2 * r:2 * r + 2], lat_mate[f, 2 * r:2 * r + 2])
            high_rows = jnp.where(lat_even, lat_mate[f, 2 * r:2 * r + 2], lat_far[f, 2 * r:2 * r + 2])
            lat_lo_buf[f, r - 2] = lat_fix(lat_lo_buf[f, r - 2], low_rows, high_rows, True)
            lat_hi_buf[f, r - 2] = lat_fix(lat_hi_buf[f, r - 2], low_rows, high_rows, False)
    copies = [pltpu.make_async_copy(d, s, sems.at[4 + i]) for i, (s, d) in enumerate(regions)]
    for c in copies:
        c.start()
    for c in copies:
        c.wait()


def add_halos(parity, out, lon_low, lon_high, lat_low, lat_high):
    fields, nlon, nlat, lev = out.shape
    hbm = pl.BlockSpec(memory_space=pl.ANY)
    return pl.pallas_call(
        halo_kernel,
        in_specs=[pl.BlockSpec(memory_space=pltpu.SMEM)] + [hbm] * 5,
        out_specs=hbm,
        out_shape=jax.ShapeDtypeStruct(out.shape, jnp.float32),
        scratch_shapes=[
            pltpu.VMEM(lon_low.shape, jnp.float32),
            pltpu.VMEM(lon_high.shape, jnp.float32),
            pltpu.VMEM(lat_low.shape, jnp.float32),
            pltpu.VMEM(lat_high.shape, jnp.float32),
            pltpu.VMEM((fields, 2, nlat, lev), jnp.float32),
            pltpu.VMEM((fields, 2, nlat, lev), jnp.float32),
            pltpu.VMEM((fields, nlon - 4, 8, lev), jnp.float32),
            pltpu.VMEM((fields, nlon - 4, 8, lev), jnp.float32),
            pltpu.SemaphoreType.DMA((8,)),
        ],
        input_output_aliases={5: 0},
    )(parity, lon_low, lon_high, lat_low, lat_high, out)


def pairings(axis, periodic):
    count = lax.axis_size(axis)
    mate = [(i, i ^ 1) for i in range(count)]
    far = []
    for i in range(1, count, 2):
        j = i + 1
        if j == count:
            if not periodic:
                continue
            j = 0
        far += [(i, j), (j, i)]
    return mate, far


def on_device(trajectory, cotangent, courant, branch, cloud_list, cloud_count):
    fields, nlon, nlat, lev = cotangent.shape
    rows = 8
    parity = jnp.stack([lax.axis_index("lon") % 2, lax.axis_index("lat") % 2]).astype(jnp.int32)
    mask = cloudy_columns(cloud_list, cloud_count, nlon, nlat, rows)
    first, lon_mate, lon_far, lat_mate, lat_far = first_pair(parity, trajectory, cotangent, branch, mask, courant, rows)
    mate, far = pairings("lon", True)
    lon_mate = lax.ppermute(lon_mate, "lon", mate)
    lon_far = lax.ppermute(lon_far, "lon", far)
    mate, far = pairings("lat", False)
    lat_mate = lax.ppermute(lat_mate, "lat", mate)
    lat_far = lax.ppermute(lat_far, "lat", far)
    out = advect(first, cotangent, courant)
    return add_halos(parity, out, lon_mate, lon_far, lat_mate, lat_far)


def solution(mesh):
    placed = (
        P(None, "lon", "lat", None),
        P(None, "lon", "lat", None),
        P(None, "lon", "lat", None),
        P("lon", "lat", None),
        P("lon", "lat", None),
        P("lon", "lat"),
    )
    return jax.shard_map(
        on_device,
        mesh=mesh,
        in_specs=placed,
        out_specs=P(None, "lon", "lat", None),
        check_vma=False,
    )
```

```python
import jax
import jax.numpy as jnp
from jax import lax
from jax.experimental import pallas as pl
from jax.experimental.pallas import tpu as pltpu
from jax.sharding import PartitionSpec as P

NEWT = 4


growth = 0.5
latent_liquid = 1.0
latent_ice = 1.3


def sat_adjoint(warmth, vapour, kinds, cot_heat, cot_vapour, cot_liquid, cot_ice):
    mixed = jax.nn.sigmoid(2.0 * warmth)
    liquid_share = jnp.where(kinds == 1, 1.0, jnp.where(kinds == 2, 0.0, mixed))
    latent = latent_liquid * liquid_share + latent_ice * (1.0 - liquid_share)
    active = (kinds > 0).astype(warmth.dtype)
    half_latent = growth * latent
    amount = jnp.zeros_like(warmth)
    saved = []
    for newton_step in range(NEWT):
        saturated = jnp.exp(growth * (warmth + latent * amount))
        inverse = 1.0 / (1.0 + half_latent * saturated)
        excess = vapour - amount - saturated
        saved.append((amount, saturated, inverse, excess))
        amount = amount + excess * inverse
    amount = active * amount
    grad_amount = latent * cot_heat - cot_vapour + liquid_share * cot_liquid + (1.0 - liquid_share) * cot_ice
    grad_share = amount * (cot_liquid - cot_ice)
    grad_latent = amount * cot_heat
    grad = active * grad_amount
    grad_heat = jnp.zeros_like(warmth)
    grad_vapour = jnp.zeros_like(warmth)
    for amount, saturated, inverse, excess in reversed(saved):
        slope = excess * inverse * inverse
        grad_sat = -grad * (inverse + half_latent * slope)
        half_sat = growth * saturated
        grad_heat = grad_heat + grad_sat * half_sat
        grad_latent = grad_latent + grad_sat * half_sat * amount - grad * slope * half_sat
        grad_vapour = grad_vapour + grad * inverse
        grad = grad * (1.0 - inverse) + grad_sat * half_latent * saturated
    grad_share = grad_share + (latent_liquid - latent_ice) * grad_latent
    mixed_kind = (kinds == 0) | (kinds == 3)
    grad_heat = grad_heat + jnp.where(mixed_kind, grad_share * 2.0 * mixed * (1.0 - mixed), 0.0)
    return (cot_heat + grad_heat, cot_vapour + grad_vapour)


def cloudy_columns(cloud_list, cloud_count, nlon, nlat, rows):
    index = cloud_list[0, 0]
    count = cloud_count[0, 0]
    slot = jnp.arange(index.shape[0], dtype=jnp.int32)
    hit = (index[:, None] == jnp.arange(nlon * nlat, dtype=jnp.int32)[None, :]) & (slot < count)[:, None]
    cloudy = jnp.any(hit, axis=0).astype(jnp.float32)
    return jnp.transpose(cloudy.reshape(nlon // rows, rows, nlat), (0, 2, 1))


def sat_kernel(traj_ref, cot_ref, kind_ref, mask_ref, cour_ref,
               out_ref, lon_mate, lon_far, lat_mate, lat_far):
    fields, rows, nlat, lev = cot_ref.shape
    step = pl.program_id(0)
    last = pl.num_programs(0) - 1
    chunk = 32
    parts = nlat // chunk
    for r in range(rows):
        after = [[None] * parts for _ in range(fields)]
        for j in range(parts):
            lat = pl.ds(j * chunk, chunk)
            cot = [cot_ref[k, r, lat, :] for k in range(4)]
            new_heat, new_vapour = sat_adjoint(
                traj_ref[0, r, lat, :], traj_ref[1, r, lat, :], kind_ref[r, lat, :], *cot
            )
            cloudy = jnp.broadcast_to(mask_ref[0, lat, r:r + 1], (chunk, lev)) > 0.0
            heat = jnp.where(cloudy, new_heat, cot[0])
            vapour = jnp.where(cloudy, new_vapour, cot[1])
            out_ref[0, r, lat, :] = heat
            out_ref[1, r, lat, :] = vapour
            after[0][j] = heat
            after[1][j] = vapour
            for f in range(2, fields):
                after[f][j] = cot_ref[f, r, lat, :]
        low_weight = cour_ref[1, r, 0:2, :]
        high_weight = cour_ref[1, r, nlat - 2:nlat, :]
        lat_even = lax.axis_index("lat") % 2 == 0
        for f in range(fields):
            bottom = low_weight * after[f][0][0:2]
            top = high_weight * after[f][parts - 1][chunk - 2:chunk]
            lat_mate[f, 2 * r:2 * r + 2, :] = jnp.where(lat_even, top, bottom)
            lat_far[f, 2 * r:2 * r + 2, :] = jnp.where(lat_even, bottom, top)
        lon_even = lax.axis_index("lon") % 2 == 0
        for edge_step, edge_rows, mate_when in ((0, range(2), jnp.logical_not(lon_even)), (last, range(rows - 2, rows), lon_even)):
            if r not in edge_rows:
                continue
            at = r - edge_rows[0]
            for target, flag in ((lon_mate, mate_when), (lon_far, jnp.logical_not(mate_when))):
                @pl.when((step == edge_step) & flag)
                def _():
                    for f in range(fields):
                        for j in range(parts):
                            lat = pl.ds(j * chunk, chunk)
                            target[f, at, lat, :] = cour_ref[0, r, lat, :] * after[f][j]


def first_pair(trajectory, cotangent, branch, mask, courant, rows):
    fields, nlon, nlat, lev = cotangent.shape
    lon_send = jax.ShapeDtypeStruct((fields, 2, nlat, lev), jnp.float32)
    lat_send = jax.ShapeDtypeStruct((fields, 2 * nlon, lev), jnp.float32)
    return pl.pallas_call(
        sat_kernel,
        grid=(nlon // rows,),
        in_specs=[
            pl.BlockSpec((2, rows, nlat, lev), lambda i: (0, i, 0, 0)),
            pl.BlockSpec((fields, rows, nlat, lev), lambda i: (0, i, 0, 0)),
            pl.BlockSpec((rows, nlat, lev), lambda i: (i, 0, 0)),
            pl.BlockSpec((1, nlat, rows), lambda i: (i, 0, 0)),
            pl.BlockSpec((2, rows, nlat, lev), lambda i: (0, i, 0, 0)),
        ],
        out_specs=[
            pl.BlockSpec((2, rows, nlat, lev), lambda i: (0, i, 0, 0)),
            pl.BlockSpec((fields, 2, nlat, lev), lambda i: (0, 0, 0, 0)),
            pl.BlockSpec((fields, 2, nlat, lev), lambda i: (0, 0, 0, 0)),
            pl.BlockSpec((fields, 2 * rows, lev), lambda i: (0, i, 0)),
            pl.BlockSpec((fields, 2 * rows, lev), lambda i: (0, i, 0)),
        ],
        out_shape=[jax.ShapeDtypeStruct((2, nlon, nlat, lev), jnp.float32), lon_send, lon_send, lat_send, lat_send],
    )(trajectory, cotangent, branch, mask, courant)


def stencil_kernel(first_hbm, cot_hbm, cour_hbm, out_hbm, field_v, cour_v, out_v, lon_pad, lat_pad, in_sems, out_sems):
    fields, nlon, nlat, lev = cot_hbm.shape
    zeros = jnp.zeros((2, nlat, lev), jnp.float32)
    cour_copy = pltpu.make_async_copy(cour_hbm, cour_v, in_sems.at[0])
    cour_copy.start()
    loads = [pltpu.make_async_copy(first_hbm, field_v.at[0:2], in_sems.at[1])]
    loads += [pltpu.make_async_copy(cot_hbm.at[f], field_v.at[f], in_sems.at[f]) for f in range(2, fields)]
    for c in loads:
        c.start()
    lon_pad[0:2] = zeros
    lon_pad[nlon + 2:nlon + 4] = zeros
    lat_pad[6:8] = zeros[0, 0:2]
    lat_pad[8 + nlat:10 + nlat] = zeros[0, 0:2]
    cour_copy.wait()
    stores = []
    for f in range(fields):
        if f == 0:
            loads[0].wait()
        elif f >= 2:
            loads[f - 1].wait()
        src = field_v.at[f]
        for r in range(nlon):
            lon_pad[r + 2] = cour_v[0, r] * src[r]
        for r in range(nlon):
            lat_pad[8:8 + nlat] = cour_v[1, r] * src[r]
            d_lat = (8.0 * (lat_pad[9:9 + nlat] - lat_pad[7:7 + nlat]) - (lat_pad[10:10 + nlat] - lat_pad[6:6 + nlat])) / 12.0
            d_lon = (8.0 * (lon_pad[r + 3] - lon_pad[r + 1]) - (lon_pad[r + 4] - lon_pad[r])) / 12.0
            out_v[f, r] = src[r] + d_lon + d_lat
        store = pltpu.make_async_copy(out_v.at[f], out_hbm.at[f], out_sems.at[f])
        store.start()
        stores.append(store)
    for store in stores:
        store.wait()


def advect(first, cotangent, courant):
    fields, nlon, nlat, lev = cotangent.shape
    size = cotangent.size * 4
    hbm = pl.BlockSpec(memory_space=pl.ANY)
    return pl.pallas_call(
        stencil_kernel,
        in_specs=[hbm, hbm, hbm],
        out_specs=hbm,
        out_shape=jax.ShapeDtypeStruct(cotangent.shape, jnp.float32),
        scratch_shapes=[
            pltpu.VMEM(cotangent.shape, jnp.float32),
            pltpu.VMEM(courant.shape, jnp.float32),
            pltpu.VMEM(cotangent.shape, jnp.float32),
            pltpu.VMEM((nlon + 4, nlat, lev), jnp.float32),
            pltpu.VMEM((nlat + 16, lev), jnp.float32),
            pltpu.SemaphoreType.DMA((fields,)),
            pltpu.SemaphoreType.DMA((fields,)),
        ],
        cost_estimate=pl.CostEstimate(flops=12 * cotangent.size, transcendentals=0, bytes_accessed=3 * size),
    )(first, cotangent, courant)


def halo_kernel(lon_mate_hbm, lon_far_hbm, lat_mate_hbm, lat_far_hbm, out_hbm, out_ref,
                lon_mate, lon_far, lat_mate, lat_far, lon_lo_buf, lon_hi_buf, lat_lo_buf, lat_hi_buf, sems):
    fields, nlon, nlat, lev = out_hbm.shape
    halos = [(lon_mate_hbm, lon_mate), (lon_far_hbm, lon_far), (lat_mate_hbm, lat_mate), (lat_far_hbm, lat_far)]
    lon_even = lax.axis_index("lon") % 2 == 0
    lat_even = lax.axis_index("lat") % 2 == 0
    regions = [
        (out_hbm.at[:, 0:2], lon_lo_buf),
        (out_hbm.at[:, nlon - 2:nlon], lon_hi_buf),
        (out_hbm.at[:, 2:nlon - 2, 0:8], lat_lo_buf),
        (out_hbm.at[:, 2:nlon - 2, nlat - 8:nlat], lat_hi_buf),
    ]
    copies = [pltpu.make_async_copy(s, d, sems.at[i]) for i, (s, d) in enumerate(halos + regions)]
    for c in copies:
        c.start()
    for c in copies:
        c.wait()
    sub = lax.broadcasted_iota(jnp.int32, (8, lev), 0)

    def lat_fix(tile, low_rows, high_rows, at_low):
        if at_low:
            row0 = (low_rows[0:1] - 8.0 * low_rows[1:2]) / 12.0
            row1 = low_rows[1:2] / 12.0
            return tile + jnp.where(sub == 0, row0, jnp.where(sub == 1, row1, 0.0))
        row6 = -high_rows[0:1] / 12.0
        row7 = (8.0 * high_rows[0:1] - high_rows[1:2]) / 12.0
        return tile + jnp.where(sub == 6, row6, jnp.where(sub == 7, row7, 0.0))

    for f in range(fields):
        lo = jnp.where(lon_even, lon_far[f], lon_mate[f])
        hi = jnp.where(lon_even, lon_mate[f], lon_far[f])
        edge_terms = [(lo[0] - 8.0 * lo[1]) / 12.0, lo[1] / 12.0, -hi[0] / 12.0, (8.0 * hi[0] - hi[1]) / 12.0]
        for k, r in enumerate((0, 1, nlon - 2, nlon - 1)):
            buf = lon_lo_buf if k < 2 else lon_hi_buf
            block = buf[f, k % 2] + edge_terms[k]
            low_rows = jnp.where(lat_even, lat_far[f, 2 * r:2 * r + 2], lat_mate[f, 2 * r:2 * r + 2])
            high_rows = jnp.where(lat_even, lat_mate[f, 2 * r:2 * r + 2], lat_far[f, 2 * r:2 * r + 2])
            buf[f, k % 2] = block
            buf[f, k % 2, 0:8] = lat_fix(block[0:8], low_rows, high_rows, True)
            buf[f, k % 2, nlat - 8:nlat] = lat_fix(block[nlat - 8:nlat], low_rows, high_rows, False)
        for r in range(2, nlon - 2):
            low_rows = jnp.where(lat_even, lat_far[f, 2 * r:2 * r + 2], lat_mate[f, 2 * r:2 * r + 2])
            high_rows = jnp.where(lat_even, lat_mate[f, 2 * r:2 * r + 2], lat_far[f, 2 * r:2 * r + 2])
            lat_lo_buf[f, r - 2] = lat_fix(lat_lo_buf[f, r - 2], low_rows, high_rows, True)
            lat_hi_buf[f, r - 2] = lat_fix(lat_hi_buf[f, r - 2], low_rows, high_rows, False)
    copies = [pltpu.make_async_copy(d, s, sems.at[4 + i]) for i, (s, d) in enumerate(regions)]
    for c in copies:
        c.start()
    for c in copies:
        c.wait()


def add_halos(out, lon_low, lon_high, lat_low, lat_high):
    fields, nlon, nlat, lev = out.shape
    hbm = pl.BlockSpec(memory_space=pl.ANY)
    return pl.pallas_call(
        halo_kernel,
        in_specs=[hbm] * 5,
        out_specs=hbm,
        out_shape=jax.ShapeDtypeStruct(out.shape, jnp.float32),
        scratch_shapes=[
            pltpu.VMEM(lon_low.shape, jnp.float32),
            pltpu.VMEM(lon_high.shape, jnp.float32),
            pltpu.VMEM(lat_low.shape, jnp.float32),
            pltpu.VMEM(lat_high.shape, jnp.float32),
            pltpu.VMEM((fields, 2, nlat, lev), jnp.float32),
            pltpu.VMEM((fields, 2, nlat, lev), jnp.float32),
            pltpu.VMEM((fields, nlon - 4, 8, lev), jnp.float32),
            pltpu.VMEM((fields, nlon - 4, 8, lev), jnp.float32),
            pltpu.SemaphoreType.DMA((8,)),
        ],
        input_output_aliases={4: 0},
    )(lon_low, lon_high, lat_low, lat_high, out)


def pairings(axis, periodic):
    count = lax.axis_size(axis)
    mate = [(i, i ^ 1) for i in range(count)]
    far = []
    for i in range(1, count, 2):
        j = i + 1
        if j == count:
            if not periodic:
                continue
            j = 0
        far += [(i, j), (j, i)]
    return mate, far


def on_device(trajectory, cotangent, courant, branch, cloud_list, cloud_count):
    fields, nlon, nlat, lev = cotangent.shape
    rows = 8
    mask = cloudy_columns(cloud_list, cloud_count, nlon, nlat, rows)
    first, lon_mate, lon_far, lat_mate, lat_far = first_pair(trajectory, cotangent, branch, mask, courant, rows)
    mate, far = pairings("lon", True)
    lon_mate = lax.ppermute(lon_mate, "lon", mate)
    lon_far = lax.ppermute(lon_far, "lon", far)
    mate, far = pairings("lat", False)
    lat_mate = lax.ppermute(lat_mate, "lat", mate)
    lat_far = lax.ppermute(lat_far, "lat", far)
    out = advect(first, cotangent, courant)
    return add_halos(out, lon_mate, lon_far, lat_mate, lat_far)


def solution(mesh):
    placed = (
        P(None, "lon", "lat", None),
        P(None, "lon", "lat", None),
        P(None, "lon", "lat", None),
        P("lon", "lat", None),
        P("lon", "lat", None),
        P("lon", "lat"),
    )
    return jax.shard_map(
        on_device,
        mesh=mesh,
        in_specs=placed,
        out_specs=P(None, "lon", "lat", None),
        check_vma=False,
    )
```

```python
import jax
import jax.numpy as jnp
from jax import lax
from jax.experimental import pallas as pl
from jax.experimental.pallas import tpu as pltpu
from jax.sharding import PartitionSpec as P

NEWT = 4


growth = 0.5
latent_liquid = 1.0
latent_ice = 1.3


def sat_adjoint(warmth, vapour, kinds, cot_heat, cot_vapour, cot_liquid, cot_ice):
    mixed = jax.nn.sigmoid(2.0 * warmth)
    liquid_share = jnp.where(kinds == 1, 1.0, jnp.where(kinds == 2, 0.0, mixed))
    latent = latent_liquid * liquid_share + latent_ice * (1.0 - liquid_share)
    active = (kinds > 0).astype(warmth.dtype)
    half_latent = growth * latent
    amount = jnp.zeros_like(warmth)
    saved = []
    for newton_step in range(NEWT):
        saturated = jnp.exp(growth * (warmth + latent * amount))
        inverse = 1.0 / (1.0 + half_latent * saturated)
        excess = vapour - amount - saturated
        saved.append((amount, saturated, inverse, excess))
        amount = amount + excess * inverse
    amount = active * amount
    grad_amount = latent * cot_heat - cot_vapour + liquid_share * cot_liquid + (1.0 - liquid_share) * cot_ice
    grad_share = amount * (cot_liquid - cot_ice)
    grad_latent = amount * cot_heat
    grad = active * grad_amount
    grad_heat = jnp.zeros_like(warmth)
    grad_vapour = jnp.zeros_like(warmth)
    for amount, saturated, inverse, excess in reversed(saved):
        slope = excess * inverse * inverse
        grad_sat = -grad * (inverse + half_latent * slope)
        half_sat = growth * saturated
        grad_heat = grad_heat + grad_sat * half_sat
        grad_latent = grad_latent + grad_sat * half_sat * amount - grad * slope * half_sat
        grad_vapour = grad_vapour + grad * inverse
        grad = grad * (1.0 - inverse) + grad_sat * half_latent * saturated
    grad_share = grad_share + (latent_liquid - latent_ice) * grad_latent
    mixed_kind = (kinds == 0) | (kinds == 3)
    grad_heat = grad_heat + jnp.where(mixed_kind, grad_share * 2.0 * mixed * (1.0 - mixed), 0.0)
    return (cot_heat + grad_heat, cot_vapour + grad_vapour)


def cloudy_columns(cloud_list, cloud_count, nlon, nlat, rows):
    index = cloud_list[0, 0]
    count = cloud_count[0, 0]
    slot = jnp.arange(index.shape[0], dtype=jnp.int32)
    hit = (index[:, None] == jnp.arange(nlon * nlat, dtype=jnp.int32)[None, :]) & (slot < count)[:, None]
    cloudy = jnp.max(jnp.where(hit, 1.0, 0.0), axis=0)
    return jnp.transpose(cloudy.reshape(nlon // rows, rows, nlat), (0, 2, 1))


def sat_kernel(traj_ref, cot_ref, kind_ref, mask_ref, cour_ref,
               out_ref, lon_mate, lon_far, lat_mate, lat_far):
    fields, rows, nlat, lev = cot_ref.shape
    step = pl.program_id(0)
    last = pl.num_programs(0) - 1
    chunk = 32
    parts = nlat // chunk
    for r in range(rows):
        after = [[None] * parts for _ in range(fields)]
        for j in range(parts):
            lat = pl.ds(j * chunk, chunk)
            cot = [cot_ref[k, r, lat, :] for k in range(4)]
            new_heat, new_vapour = sat_adjoint(
                traj_ref[0, r, lat, :], traj_ref[1, r, lat, :], kind_ref[r, lat, :], *cot
            )
            cloudy = jnp.broadcast_to(mask_ref[0, lat, r:r + 1], (chunk, lev)) > 0.0
            heat = jnp.where(cloudy, new_heat, cot[0])
            vapour = jnp.where(cloudy, new_vapour, cot[1])
            out_ref[0, r, lat, :] = heat
            out_ref[1, r, lat, :] = vapour
            after[0][j] = heat
            after[1][j] = vapour
            for f in range(2, fields):
                after[f][j] = cot_ref[f, r, lat, :]
        low_weight = cour_ref[1, r, 0:2, :]
        high_weight = cour_ref[1, r, nlat - 2:nlat, :]
        lat_even = lax.axis_index("lat") % 2 == 0
        for f in range(fields):
            bottom = low_weight * after[f][0][0:2]
            top = high_weight * after[f][parts - 1][chunk - 2:chunk]
            lat_mate[f, 2 * r:2 * r + 2, :] = jnp.where(lat_even, top, bottom)
            lat_far[f, 2 * r:2 * r + 2, :] = jnp.where(lat_even, bottom, top)
        lon_even = lax.axis_index("lon") % 2 == 0
        for edge_step, edge_rows, mate_when in ((0, range(2), jnp.logical_not(lon_even)), (last, range(rows - 2, rows), lon_even)):
            if r not in edge_rows:
                continue
            at = r - edge_rows[0]
            for target, flag in ((lon_mate, mate_when), (lon_far, jnp.logical_not(mate_when))):
                @pl.when((step == edge_step) & flag)
                def _():
                    for f in range(fields):
                        for j in range(parts):
                            lat = pl.ds(j * chunk, chunk)
                            target[f, at, lat, :] = cour_ref[0, r, lat, :] * after[f][j]


def first_pair(trajectory, cotangent, branch, mask, courant, rows):
    fields, nlon, nlat, lev = cotangent.shape
    lon_send = jax.ShapeDtypeStruct((fields, 2, nlat, lev), jnp.float32)
    lat_send = jax.ShapeDtypeStruct((fields, 2 * nlon, lev), jnp.float32)
    return pl.pallas_call(
        sat_kernel,
        grid=(nlon // rows,),
        in_specs=[
            pl.BlockSpec((2, rows, nlat, lev), lambda i: (0, i, 0, 0)),
            pl.BlockSpec((fields, rows, nlat, lev), lambda i: (0, i, 0, 0)),
            pl.BlockSpec((rows, nlat, lev), lambda i: (i, 0, 0)),
            pl.BlockSpec((1, nlat, rows), lambda i: (i, 0, 0)),
            pl.BlockSpec((2, rows, nlat, lev), lambda i: (0, i, 0, 0)),
        ],
        out_specs=[
            pl.BlockSpec((2, rows, nlat, lev), lambda i: (0, i, 0, 0)),
            pl.BlockSpec((fields, 2, nlat, lev), lambda i: (0, 0, 0, 0)),
            pl.BlockSpec((fields, 2, nlat, lev), lambda i: (0, 0, 0, 0)),
            pl.BlockSpec((fields, 2 * rows, lev), lambda i: (0, i, 0)),
            pl.BlockSpec((fields, 2 * rows, lev), lambda i: (0, i, 0)),
        ],
        out_shape=[jax.ShapeDtypeStruct((2, nlon, nlat, lev), jnp.float32), lon_send, lon_send, lat_send, lat_send],
    )(trajectory, cotangent, branch, mask, courant)


def stencil_kernel(first_hbm, cot_hbm, cour_hbm, out_hbm, field_v, cour_v, out_v, lon_pad, lat_pad, in_sems, out_sems):
    fields, nlon, nlat, lev = cot_hbm.shape
    zeros = jnp.zeros((2, nlat, lev), jnp.float32)
    cour_copy = pltpu.make_async_copy(cour_hbm, cour_v, in_sems.at[0])
    cour_copy.start()
    loads = [pltpu.make_async_copy(first_hbm, field_v.at[0:2], in_sems.at[1])]
    loads += [pltpu.make_async_copy(cot_hbm.at[f], field_v.at[f], in_sems.at[f]) for f in range(2, fields)]
    for c in loads:
        c.start()
    lon_pad[0:2] = zeros
    lon_pad[nlon + 2:nlon + 4] = zeros
    lat_pad[6:8] = zeros[0, 0:2]
    lat_pad[8 + nlat:10 + nlat] = zeros[0, 0:2]
    cour_copy.wait()
    stores = []
    for f in range(fields):
        if f == 0:
            loads[0].wait()
        elif f >= 2:
            loads[f - 1].wait()
        src = field_v.at[f]
        for r in range(nlon):
            lon_pad[r + 2] = cour_v[0, r] * src[r]
        for r in range(nlon):
            lat_pad[8:8 + nlat] = cour_v[1, r] * src[r]
            d_lat = (8.0 * (lat_pad[9:9 + nlat] - lat_pad[7:7 + nlat]) - (lat_pad[10:10 + nlat] - lat_pad[6:6 + nlat])) / 12.0
            d_lon = (8.0 * (lon_pad[r + 3] - lon_pad[r + 1]) - (lon_pad[r + 4] - lon_pad[r])) / 12.0
            out_v[f, r] = src[r] + d_lon + d_lat
        store = pltpu.make_async_copy(out_v.at[f], out_hbm.at[f], out_sems.at[f])
        store.start()
        stores.append(store)
    for store in stores:
        store.wait()


def advect(first, cotangent, courant):
    fields, nlon, nlat, lev = cotangent.shape
    size = cotangent.size * 4
    hbm = pl.BlockSpec(memory_space=pl.ANY)
    return pl.pallas_call(
        stencil_kernel,
        in_specs=[hbm, hbm, hbm],
        out_specs=hbm,
        out_shape=jax.ShapeDtypeStruct(cotangent.shape, jnp.float32),
        scratch_shapes=[
            pltpu.VMEM(cotangent.shape, jnp.float32),
            pltpu.VMEM(courant.shape, jnp.float32),
            pltpu.VMEM(cotangent.shape, jnp.float32),
            pltpu.VMEM((nlon + 4, nlat, lev), jnp.float32),
            pltpu.VMEM((nlat + 16, lev), jnp.float32),
            pltpu.SemaphoreType.DMA((fields,)),
            pltpu.SemaphoreType.DMA((fields,)),
        ],
        cost_estimate=pl.CostEstimate(flops=12 * cotangent.size, transcendentals=0, bytes_accessed=3 * size),
    )(first, cotangent, courant)


def halo_kernel(lon_mate_hbm, lon_far_hbm, lat_mate_hbm, lat_far_hbm, out_hbm, out_ref,
                lon_mate, lon_far, lat_mate, lat_far, lon_lo_buf, lon_hi_buf, lat_lo_buf, lat_hi_buf, sems):
    fields, nlon, nlat, lev = out_hbm.shape
    halos = [(lon_mate_hbm, lon_mate), (lon_far_hbm, lon_far), (lat_mate_hbm, lat_mate), (lat_far_hbm, lat_far)]
    lon_even = lax.axis_index("lon") % 2 == 0
    lat_even = lax.axis_index("lat") % 2 == 0
    regions = [
        (out_hbm.at[:, 0:2], lon_lo_buf),
        (out_hbm.at[:, nlon - 2:nlon], lon_hi_buf),
        (out_hbm.at[:, 2:nlon - 2, 0:8], lat_lo_buf),
        (out_hbm.at[:, 2:nlon - 2, nlat - 8:nlat], lat_hi_buf),
    ]
    copies = [pltpu.make_async_copy(s, d, sems.at[i]) for i, (s, d) in enumerate(halos + regions)]
    for c in copies:
        c.start()
    for c in copies:
        c.wait()
    sub = lax.broadcasted_iota(jnp.int32, (8, lev), 0)

    def lat_fix(tile, low_rows, high_rows, at_low):
        if at_low:
            row0 = (low_rows[0:1] - 8.0 * low_rows[1:2]) / 12.0
            row1 = low_rows[1:2] / 12.0
            return tile + jnp.where(sub == 0, row0, jnp.where(sub == 1, row1, 0.0))
        row6 = -high_rows[0:1] / 12.0
        row7 = (8.0 * high_rows[0:1] - high_rows[1:2]) / 12.0
        return tile + jnp.where(sub == 6, row6, jnp.where(sub == 7, row7, 0.0))

    for f in range(fields):
        lo = jnp.where(lon_even, lon_far[f], lon_mate[f])
        hi = jnp.where(lon_even, lon_mate[f], lon_far[f])
        edge_terms = [(lo[0] - 8.0 * lo[1]) / 12.0, lo[1] / 12.0, -hi[0] / 12.0, (8.0 * hi[0] - hi[1]) / 12.0]
        for k, r in enumerate((0, 1, nlon - 2, nlon - 1)):
            buf = lon_lo_buf if k < 2 else lon_hi_buf
            block = buf[f, k % 2] + edge_terms[k]
            low_rows = jnp.where(lat_even, lat_far[f, 2 * r:2 * r + 2], lat_mate[f, 2 * r:2 * r + 2])
            high_rows = jnp.where(lat_even, lat_mate[f, 2 * r:2 * r + 2], lat_far[f, 2 * r:2 * r + 2])
            buf[f, k % 2] = block
            buf[f, k % 2, 0:8] = lat_fix(block[0:8], low_rows, high_rows, True)
            buf[f, k % 2, nlat - 8:nlat] = lat_fix(block[nlat - 8:nlat], low_rows, high_rows, False)
        for r in range(2, nlon - 2):
            low_rows = jnp.where(lat_even, lat_far[f, 2 * r:2 * r + 2], lat_mate[f, 2 * r:2 * r + 2])
            high_rows = jnp.where(lat_even, lat_mate[f, 2 * r:2 * r + 2], lat_far[f, 2 * r:2 * r + 2])
            lat_lo_buf[f, r - 2] = lat_fix(lat_lo_buf[f, r - 2], low_rows, high_rows, True)
            lat_hi_buf[f, r - 2] = lat_fix(lat_hi_buf[f, r - 2], low_rows, high_rows, False)
    copies = [pltpu.make_async_copy(d, s, sems.at[4 + i]) for i, (s, d) in enumerate(regions)]
    for c in copies:
        c.start()
    for c in copies:
        c.wait()


def add_halos(out, lon_low, lon_high, lat_low, lat_high):
    fields, nlon, nlat, lev = out.shape
    hbm = pl.BlockSpec(memory_space=pl.ANY)
    return pl.pallas_call(
        halo_kernel,
        in_specs=[hbm] * 5,
        out_specs=hbm,
        out_shape=jax.ShapeDtypeStruct(out.shape, jnp.float32),
        scratch_shapes=[
            pltpu.VMEM(lon_low.shape, jnp.float32),
            pltpu.VMEM(lon_high.shape, jnp.float32),
            pltpu.VMEM(lat_low.shape, jnp.float32),
            pltpu.VMEM(lat_high.shape, jnp.float32),
            pltpu.VMEM((fields, 2, nlat, lev), jnp.float32),
            pltpu.VMEM((fields, 2, nlat, lev), jnp.float32),
            pltpu.VMEM((fields, nlon - 4, 8, lev), jnp.float32),
            pltpu.VMEM((fields, nlon - 4, 8, lev), jnp.float32),
            pltpu.SemaphoreType.DMA((8,)),
        ],
        input_output_aliases={4: 0},
    )(lon_low, lon_high, lat_low, lat_high, out)


def pairings(axis, periodic):
    count = lax.axis_size(axis)
    mate = [(i, i ^ 1) for i in range(count)]
    far = []
    for i in range(1, count, 2):
        j = i + 1
        if j == count:
            if not periodic:
                continue
            j = 0
        far += [(i, j), (j, i)]
    return mate, far


def on_device(trajectory, cotangent, courant, branch, cloud_list, cloud_count):
    fields, nlon, nlat, lev = cotangent.shape
    rows = 8
    mask = cloudy_columns(cloud_list, cloud_count, nlon, nlat, rows)
    first, lon_mate, lon_far, lat_mate, lat_far = first_pair(trajectory, cotangent, branch, mask, courant, rows)
    mate, far = pairings("lon", True)
    lon_mate = lax.ppermute(lon_mate, "lon", mate)
    lon_far = lax.ppermute(lon_far, "lon", far)
    mate, far = pairings("lat", False)
    lat_mate = lax.ppermute(lat_mate, "lat", mate)
    lat_far = lax.ppermute(lat_far, "lat", far)
    out = advect(first, cotangent, courant)
    return add_halos(out, lon_mate, lon_far, lat_mate, lat_far)


def solution(mesh):
    placed = (
        P(None, "lon", "lat", None),
        P(None, "lon", "lat", None),
        P(None, "lon", "lat", None),
        P("lon", "lat", None),
        P("lon", "lat", None),
        P("lon", "lat"),
    )
    return jax.shard_map(
        on_device,
        mesh=mesh,
        in_specs=placed,
        out_specs=P(None, "lon", "lat", None),
        check_vma=False,
    )
```

```python
import jax
import jax.numpy as jnp
from jax import lax
from jax.experimental import pallas as pl
from jax.experimental.pallas import tpu as pltpu
from jax.sharding import PartitionSpec as P

NEWT = 4


growth = 0.5
latent_liquid = 1.0
latent_ice = 1.3


def sat_adjoint(warmth, vapour, kinds, cot_heat, cot_vapour, cot_liquid, cot_ice):
    mixed = jax.nn.sigmoid(2.0 * warmth)
    liquid_share = jnp.where(kinds == 1, 1.0, jnp.where(kinds == 2, 0.0, mixed))
    latent = latent_liquid * liquid_share + latent_ice * (1.0 - liquid_share)
    active = (kinds > 0).astype(warmth.dtype)
    half_latent = growth * latent
    amount = jnp.zeros_like(warmth)
    saved = []
    for newton_step in range(NEWT):
        saturated = jnp.exp(growth * (warmth + latent * amount))
        inverse = 1.0 / (1.0 + half_latent * saturated)
        excess = vapour - amount - saturated
        saved.append((amount, saturated, inverse, excess))
        amount = amount + excess * inverse
    amount = active * amount
    grad_amount = latent * cot_heat - cot_vapour + liquid_share * cot_liquid + (1.0 - liquid_share) * cot_ice
    grad_share = amount * (cot_liquid - cot_ice)
    grad_latent = amount * cot_heat
    grad = active * grad_amount
    grad_heat = jnp.zeros_like(warmth)
    grad_vapour = jnp.zeros_like(warmth)
    for amount, saturated, inverse, excess in reversed(saved):
        slope = excess * inverse * inverse
        grad_sat = -grad * (inverse + half_latent * slope)
        half_sat = growth * saturated
        grad_heat = grad_heat + grad_sat * half_sat
        grad_latent = grad_latent + grad_sat * half_sat * amount - grad * slope * half_sat
        grad_vapour = grad_vapour + grad * inverse
        grad = grad * (1.0 - inverse) + grad_sat * half_latent * saturated
    grad_share = grad_share + (latent_liquid - latent_ice) * grad_latent
    mixed_kind = (kinds == 0) | (kinds == 3)
    grad_heat = grad_heat + jnp.where(mixed_kind, grad_share * 2.0 * mixed * (1.0 - mixed), 0.0)
    return (cot_heat + grad_heat, cot_vapour + grad_vapour)


def cloudy_columns(cloud_list, cloud_count, nlon, nlat, rows):
    index = cloud_list[0, 0]
    count = cloud_count[0, 0]
    slot = jnp.arange(index.shape[0], dtype=jnp.int32)
    hit = (index[:, None] == jnp.arange(nlon * nlat, dtype=jnp.int32)[None, :]) & (slot < count)[:, None]
    cloudy = jnp.any(hit, axis=0).astype(jnp.float32)
    return jnp.transpose(cloudy.reshape(nlon // rows, rows, nlat), (0, 2, 1))


def sat_kernel(traj_ref, cot_ref, kind_ref, mask_ref, cour_ref,
               out_ref, lon_mate, lon_far, lat_mate, lat_far):
    fields, rows, nlat, lev = cot_ref.shape
    step = pl.program_id(0)
    last = pl.num_programs(0) - 1
    chunk = 32
    parts = nlat // chunk
    for r in range(rows):
        after = [[None] * parts for _ in range(fields)]
        for j in range(parts):
            lat = pl.ds(j * chunk, chunk)
            cot = [cot_ref[k, r, lat, :] for k in range(4)]
            new_heat, new_vapour = sat_adjoint(
                traj_ref[0, r, lat, :], traj_ref[1, r, lat, :], kind_ref[r, lat, :], *cot
            )
            cloudy = jnp.broadcast_to(mask_ref[0, lat, r:r + 1], (chunk, lev)) > 0.0
            heat = jnp.where(cloudy, new_heat, cot[0])
            vapour = jnp.where(cloudy, new_vapour, cot[1])
            out_ref[0, r, lat, :] = heat
            out_ref[1, r, lat, :] = vapour
            after[0][j] = heat
            after[1][j] = vapour
            for f in range(2, fields):
                after[f][j] = cot_ref[f, r, lat, :]
        low_weight = cour_ref[1, r, 0:2, :]
        high_weight = cour_ref[1, r, nlat - 2:nlat, :]
        lat_even = lax.axis_index("lat") % 2 == 0
        for f in range(fields):
            bottom = low_weight * after[f][0][0:2]
            top = high_weight * after[f][parts - 1][chunk - 2:chunk]
            lat_mate[f, 2 * r:2 * r + 2, :] = jnp.where(lat_even, top, bottom)
            lat_far[f, 2 * r:2 * r + 2, :] = jnp.where(lat_even, bottom, top)
        lon_even = lax.axis_index("lon") % 2 == 0
        for edge_step, edge_rows, mate_when in ((0, range(2), jnp.logical_not(lon_even)), (last, range(rows - 2, rows), lon_even)):
            if r not in edge_rows:
                continue
            at = r - edge_rows[0]
            for target, flag in ((lon_mate, mate_when), (lon_far, jnp.logical_not(mate_when))):
                @pl.when((step == edge_step) & flag)
                def _():
                    for f in range(fields):
                        for j in range(parts):
                            lat = pl.ds(j * chunk, chunk)
                            target[f, at, lat, :] = cour_ref[0, r, lat, :] * after[f][j]


def first_pair(trajectory, cotangent, branch, mask, courant, rows):
    fields, nlon, nlat, lev = cotangent.shape
    lon_send = jax.ShapeDtypeStruct((fields, 2, nlat, lev), jnp.float32)
    lat_send = jax.ShapeDtypeStruct((fields, 2 * nlon, lev), jnp.float32)
    return pl.pallas_call(
        sat_kernel,
        grid=(nlon // rows,),
        in_specs=[
            pl.BlockSpec((2, rows, nlat, lev), lambda i: (0, i, 0, 0)),
            pl.BlockSpec((fields, rows, nlat, lev), lambda i: (0, i, 0, 0)),
            pl.BlockSpec((rows, nlat, lev), lambda i: (i, 0, 0)),
            pl.BlockSpec((1, nlat, rows), lambda i: (i, 0, 0)),
            pl.BlockSpec((2, rows, nlat, lev), lambda i: (0, i, 0, 0)),
        ],
        out_specs=[
            pl.BlockSpec((2, rows, nlat, lev), lambda i: (0, i, 0, 0)),
            pl.BlockSpec((fields, 2, nlat, lev), lambda i: (0, 0, 0, 0)),
            pl.BlockSpec((fields, 2, nlat, lev), lambda i: (0, 0, 0, 0)),
            pl.BlockSpec((fields, 2 * rows, lev), lambda i: (0, i, 0)),
            pl.BlockSpec((fields, 2 * rows, lev), lambda i: (0, i, 0)),
        ],
        out_shape=[jax.ShapeDtypeStruct((2, nlon, nlat, lev), jnp.float32), lon_send, lon_send, lat_send, lat_send],
    )(trajectory, cotangent, branch, mask, courant)


def stencil_kernel(first_hbm, cot_hbm, cour_hbm, out_hbm, field_v, cour_v, out_v, lon_pad, lat_pad, in_sems, out_sems):
    fields, nlon, nlat, lev = cot_hbm.shape
    zeros = jnp.zeros((2, nlat, lev), jnp.float32)
    cour_copy = pltpu.make_async_copy(cour_hbm, cour_v, in_sems.at[0])
    cour_copy.start()
    loads = [pltpu.make_async_copy(first_hbm, field_v.at[0:2], in_sems.at[1])]
    loads += [pltpu.make_async_copy(cot_hbm.at[f], field_v.at[f], in_sems.at[f]) for f in range(2, fields)]
    for c in loads:
        c.start()
    lon_pad[0:2] = zeros
    lon_pad[nlon + 2:nlon + 4] = zeros
    lat_pad[6:8] = zeros[0, 0:2]
    lat_pad[8 + nlat:10 + nlat] = zeros[0, 0:2]
    cour_copy.wait()
    stores = []
    for f in range(fields):
        if f == 0:
            loads[0].wait()
        elif f >= 2:
            loads[f - 1].wait()
        src = field_v.at[f]
        for r in range(nlon):
            lon_pad[r + 2] = cour_v[0, r] * src[r]
        for r in range(nlon):
            lat_pad[8:8 + nlat] = cour_v[1, r] * src[r]
            d_lat = (8.0 * (lat_pad[9:9 + nlat] - lat_pad[7:7 + nlat]) - (lat_pad[10:10 + nlat] - lat_pad[6:6 + nlat])) / 12.0
            d_lon = (8.0 * (lon_pad[r + 3] - lon_pad[r + 1]) - (lon_pad[r + 4] - lon_pad[r])) / 12.0
            out_v[f, r] = src[r] + d_lon + d_lat
        store = pltpu.make_async_copy(out_v.at[f], out_hbm.at[f], out_sems.at[f])
        store.start()
        stores.append(store)
    for store in stores:
        store.wait()


def advect(first, cotangent, courant):
    fields, nlon, nlat, lev = cotangent.shape
    size = cotangent.size * 4
    hbm = pl.BlockSpec(memory_space=pl.ANY)
    return pl.pallas_call(
        stencil_kernel,
        in_specs=[hbm, hbm, hbm],
        out_specs=hbm,
        out_shape=jax.ShapeDtypeStruct(cotangent.shape, jnp.float32),
        scratch_shapes=[
            pltpu.VMEM(cotangent.shape, jnp.float32),
            pltpu.VMEM(courant.shape, jnp.float32),
            pltpu.VMEM(cotangent.shape, jnp.float32),
            pltpu.VMEM((nlon + 4, nlat, lev), jnp.float32),
            pltpu.VMEM((nlat + 16, lev), jnp.float32),
            pltpu.SemaphoreType.DMA((fields,)),
            pltpu.SemaphoreType.DMA((fields,)),
        ],
        cost_estimate=pl.CostEstimate(flops=12 * cotangent.size, transcendentals=0, bytes_accessed=3 * size),
    )(first, cotangent, courant)


def halo_kernel(lon_mate_hbm, lon_far_hbm, lat_mate_hbm, lat_far_hbm, out_hbm, out_ref,
                lon_mate, lon_far, lat_mate, lat_far, lon_lo_buf, lon_hi_buf, lat_lo_buf, lat_hi_buf, sems):
    fields, nlon, nlat, lev = out_hbm.shape
    halos = [(lon_mate_hbm, lon_mate), (lon_far_hbm, lon_far), (lat_mate_hbm, lat_mate), (lat_far_hbm, lat_far)]
    lon_even = lax.axis_index("lon") % 2 == 0
    lat_even = lax.axis_index("lat") % 2 == 0
    regions = [
        (out_hbm.at[:, 0:2], lon_lo_buf),
        (out_hbm.at[:, nlon - 2:nlon], lon_hi_buf),
        (out_hbm.at[:, 2:nlon - 2, 0:8], lat_lo_buf),
        (out_hbm.at[:, 2:nlon - 2, nlat - 8:nlat], lat_hi_buf),
    ]
    copies = [pltpu.make_async_copy(s, d, sems.at[i]) for i, (s, d) in enumerate(halos + regions)]
    for c in copies:
        c.start()
    for c in copies:
        c.wait()
    sub = lax.broadcasted_iota(jnp.int32, (8, lev), 0)

    def lat_fix(tile, low_rows, high_rows, at_low):
        if at_low:
            row0 = (low_rows[0:1] - 8.0 * low_rows[1:2]) * (1.0 / 12.0)
            row1 = low_rows[1:2] * (1.0 / 12.0)
            return tile + jnp.where(sub == 0, row0, jnp.where(sub == 1, row1, 0.0))
        row6 = -high_rows[0:1] * (1.0 / 12.0)
        row7 = (8.0 * high_rows[0:1] - high_rows[1:2]) * (1.0 / 12.0)
        return tile + jnp.where(sub == 6, row6, jnp.where(sub == 7, row7, 0.0))

    for f in range(fields):
        lo = jnp.where(lon_even, lon_far[f], lon_mate[f])
        hi = jnp.where(lon_even, lon_mate[f], lon_far[f])
        edge_terms = [(lo[0] - 8.0 * lo[1]) * (1.0 / 12.0), lo[1] * (1.0 / 12.0), -hi[0] * (1.0 / 12.0), (8.0 * hi[0] - hi[1]) * (1.0 / 12.0)]
        for k, r in enumerate((0, 1, nlon - 2, nlon - 1)):
            buf = lon_lo_buf if k < 2 else lon_hi_buf
            block = buf[f, k % 2] + edge_terms[k]
            low_rows = jnp.where(lat_even, lat_far[f, 2 * r:2 * r + 2], lat_mate[f, 2 * r:2 * r + 2])
            high_rows = jnp.where(lat_even, lat_mate[f, 2 * r:2 * r + 2], lat_far[f, 2 * r:2 * r + 2])
            buf[f, k % 2] = block
            buf[f, k % 2, 0:8] = lat_fix(block[0:8], low_rows, high_rows, True)
            buf[f, k % 2, nlat - 8:nlat] = lat_fix(block[nlat - 8:nlat], low_rows, high_rows, False)
        for r in range(2, nlon - 2):
            low_rows = jnp.where(lat_even, lat_far[f, 2 * r:2 * r + 2], lat_mate[f, 2 * r:2 * r + 2])
            high_rows = jnp.where(lat_even, lat_mate[f, 2 * r:2 * r + 2], lat_far[f, 2 * r:2 * r + 2])
            lat_lo_buf[f, r - 2] = lat_fix(lat_lo_buf[f, r - 2], low_rows, high_rows, True)
            lat_hi_buf[f, r - 2] = lat_fix(lat_hi_buf[f, r - 2], low_rows, high_rows, False)
    copies = [pltpu.make_async_copy(d, s, sems.at[4 + i]) for i, (s, d) in enumerate(regions)]
    for c in copies:
        c.start()
    for c in copies:
        c.wait()


def add_halos(out, lon_low, lon_high, lat_low, lat_high):
    fields, nlon, nlat, lev = out.shape
    hbm = pl.BlockSpec(memory_space=pl.ANY)
    return pl.pallas_call(
        halo_kernel,
        in_specs=[hbm] * 5,
        out_specs=hbm,
        out_shape=jax.ShapeDtypeStruct(out.shape, jnp.float32),
        scratch_shapes=[
            pltpu.VMEM(lon_low.shape, jnp.float32),
            pltpu.VMEM(lon_high.shape, jnp.float32),
            pltpu.VMEM(lat_low.shape, jnp.float32),
            pltpu.VMEM(lat_high.shape, jnp.float32),
            pltpu.VMEM((fields, 2, nlat, lev), jnp.float32),
            pltpu.VMEM((fields, 2, nlat, lev), jnp.float32),
            pltpu.VMEM((fields, nlon - 4, 8, lev), jnp.float32),
            pltpu.VMEM((fields, nlon - 4, 8, lev), jnp.float32),
            pltpu.SemaphoreType.DMA((8,)),
        ],
        input_output_aliases={4: 0},
    )(lon_low, lon_high, lat_low, lat_high, out)


def pairings(axis, periodic):
    count = lax.axis_size(axis)
    mate = [(i, i ^ 1) for i in range(count)]
    far = []
    for i in range(1, count, 2):
        j = i + 1
        if j == count:
            if not periodic:
                continue
            j = 0
        far += [(i, j), (j, i)]
    return mate, far


def on_device(trajectory, cotangent, courant, branch, cloud_list, cloud_count):
    fields, nlon, nlat, lev = cotangent.shape
    rows = 8
    mask = cloudy_columns(cloud_list, cloud_count, nlon, nlat, rows)
    first, lon_mate, lon_far, lat_mate, lat_far = first_pair(trajectory, cotangent, branch, mask, courant, rows)
    mate, far = pairings("lon", True)
    lon_mate = lax.ppermute(lon_mate, "lon", mate)
    lon_far = lax.ppermute(lon_far, "lon", far)
    mate, far = pairings("lat", False)
    lat_mate = lax.ppermute(lat_mate, "lat", mate)
    lat_far = lax.ppermute(lat_far, "lat", far)
    out = advect(first, cotangent, courant)
    return add_halos(out, lon_mate, lon_far, lat_mate, lat_far)


def solution(mesh):
    placed = (
        P(None, "lon", "lat", None),
        P(None, "lon", "lat", None),
        P(None, "lon", "lat", None),
        P("lon", "lat", None),
        P("lon", "lat", None),
        P("lon", "lat"),
    )
    return jax.shard_map(
        on_device,
        mesh=mesh,
        in_specs=placed,
        out_specs=P(None, "lon", "lat", None),
        check_vma=False,
    )
```
